256 devices in a mesh: gx: 32 (over z, x_hi, core), gy: 8 (over x_lo, y).
Axes of the slice: x: 4 (x_hi: 2, x_lo: 2; x = x_hi * 2 + x_lo), y: 4, z: 8, core: 2. Of those that a mesh axis runs over, the one named last changes fastest.
Arguments:
- magnet: float32 [3, 256, 128, 128], P(None, 'gx', 'gy'), may hold values from -5 to 5
- grain_ids: int32 [256, 128, 128], P('gx', 'gy'), may hold values from 0 to 3
- exch_table: float32 [4], replicated, may hold values from 0.05 to 0.4
- sat_table: float32 [4], replicated, may hold values from 0.5 to 4
- surface_map: int32 [64, 8, 128], P('gx', 'gy'), may hold values from 0 to 127, each once within a row
- near_list: int32 [32, 16, 8], P('gx', 'gy'), may hold values from 0 to 15
- near_blocks: bfloat16 [32, 16, 8, 128, 128], P('gx', 'gy'), may hold values from -0.1875 to 0.1875
Outputs:
- field: float32 [3, 256, 128, 128], P(None, 'gx', 'gy')
- potential: float32 [256, 128, 128], P('gx', 'gy')
The draws below stay inside these ranges and needn't reach their ends.
All inputs are finite; a program needn't handle non-finite values.
Results may differ from the reference program's by a relative error of at most 0.0019.
Values may be sent and summed in bfloat16 or wider, within the bound.
No kernel may reach another device: no remote copies, remote signals or barrier semaphores. Data moves between devices by JAX's collectives and lax.ppermute only.
A program may use at most 64 MiB of HBM per device.

```python
import math
import jax
import jax.numpy as jnp
from jax import lax

CX = 8
CY = 16
NODES = 128
KB = 8
SWEEPS = 8
EXT_SWEEPS = 4
NMAT = 4
PANELS = 2
NX = 256
NY = 128
NZ = 128
N_GX = 32
N_GY = 8


def plant(array, rng, low, largest):
    spot = [jax.random.randint(jax.random.fold_in(rng, axis), (), 0, length) for axis, length in enumerate(array.shape)]
    main_axis = array.shape.index(max(array.shape))
    beside = spot[:main_axis] + [(spot[main_axis] + 1) % array.shape[main_axis]] + spot[main_axis + 1:]
    return array.at[tuple(spot)].set(low).at[tuple(beside)].set(largest)


def level_of(stream_key, shape, shards, least, top_value):
    def one(dim, parts):
        steps = jax.random.uniform(jax.random.fold_in(jax.random.fold_in(stream_key, 6), dim), (parts,), jnp.float32, least / len(shards), top_value / len(shards))
        return jnp.repeat(jnp.exp(steps), shape[dim] // parts).reshape((-1,) + (1,) * (len(shape) - dim - 1))

    factor_of = one(*shards[0])
    for cut in shards[1:]:
        factor_of = factor_of * one(*cut)
    return factor_of


def scatter_about(own_key, extent, scale, reach, split=(), kind=jnp.bfloat16):
    values = scale * jax.random.normal(own_key, extent, jnp.float32)
    if split:
        values = values * level_of(own_key, extent, split, -0.22, 0.18)
    return jnp.clip(values, -reach, reach).astype(kind)


def setup_inputs(seed: int = 0) -> dict:
    key_list = jax.random.split(jax.random.key(seed), 8)
    magnet = scatter_about(key_list[0], (3, NX, NY, NZ), 1.0, 5.0, ((1, 32), (2, 8)), jnp.float32)
    grain_ids = plant(jax.random.randint(key_list[1], (NX, NY, NZ), 0, NMAT), jax.random.fold_in(key_list[1], 1), 0, NMAT - 1).astype(jnp.int32)
    exch_table = jnp.clip(jnp.exp(jax.random.uniform(key_list[2], (NMAT,), jnp.float32, math.log(0.05), math.log(0.4))), 0.05, 0.4)
    sat_table = jnp.clip(jnp.exp(jax.random.uniform(key_list[3], (NMAT,), jnp.float32, math.log(0.5), math.log(4.0))), 0.5, 4.0)
    surface_map = jax.vmap(lambda own: jax.random.permutation(own, CX * CY))(jax.random.split(key_list[4], (2 * N_GX) * N_GY)).reshape((2 * N_GX, N_GY, CX * CY)).astype(jnp.int32)
    near_list = plant(jax.random.randint(key_list[5], (N_GX, N_GY * PANELS, KB), 0, N_GY * PANELS), jax.random.fold_in(key_list[5], 1), 0, (N_GY * PANELS) - 1).astype(jnp.int32)
    near_blocks = scatter_about(key_list[6], (N_GX, N_GY * PANELS, KB, NODES, NODES), (NODES * KB) ** -0.5, 0.1875, ((0, 32), (1, 8)))
    return dict(magnet=magnet, grain_ids=grain_ids, exch_table=exch_table, sat_table=sat_table, surface_map=surface_map, near_list=near_list, near_blocks=near_blocks)


SCREEN = 0.25
DIAG = 6.0 + SCREEN


def neighbours(field_in):
    padded = jnp.pad(field_in, ((0, 0), (1, 1), (1, 1), (1, 1)))
    total = padded[:, 2:, 1:-1, 1:-1] + padded[:, :-2, 1:-1, 1:-1]
    total = total + padded[:, 1:-1, 2:, 1:-1] + padded[:, 1:-1, :-2, 1:-1]
    total = total + padded[:, 1:-1, 1:-1, 2:] + padded[:, 1:-1, 1:-1, :-2]
    return total


def lookup(grain_ids, table):
    result = jnp.zeros(grain_ids.shape, jnp.float32)
    for index in range(NMAT):
        result = result + (grain_ids == index).astype(jnp.float32) * table[index]
    return result


def reset_planes(values, lower, upper):
    values = values.at[:, :, :, 0].set(lower)
    return values.at[:, :, :, -1].set(upper)


def reference(magnet, grain_ids, exch_table, sat_table, surface_map, near_list, near_blocks):
    exch_coef = lookup(grain_ids, exch_table)
    sat_coef = lookup(grain_ids, sat_table)
    laplace = neighbours(magnet) - 6.0 * magnet
    padded = jnp.pad(magnet, ((0, 0), (1, 1), (1, 1), (1, 1)))
    diverge = (padded[0, 2:, 1:-1, 1:-1] - padded[0, :-2, 1:-1, 1:-1]
               + padded[1, 1:-1, 2:, 1:-1] - padded[1, 1:-1, :-2, 1:-1]
               + padded[2, 1:-1, 1:-1, 2:] - padded[2, 1:-1, 1:-1, :-2]) * 0.5
    source = (-sat_coef * diverge)[None]
    scalar = jnp.zeros(source.shape, jnp.float32)
    for sweep in range(SWEEPS):
        scalar = (neighbours(scalar) + source) / DIAG
    faces = jnp.stack([scalar[0, :, :, 0], scalar[0, :, :, -1]])
    blocked = faces.reshape(2, N_GX, CX, N_GY, CY).transpose(1, 3, 0, 2, 4).reshape(N_GX, N_GY, 2, CX * CY)
    node_map = surface_map.reshape(N_GX, 2, N_GY, CX * CY).transpose(0, 2, 1, 3)
    nodes = jnp.take_along_axis(blocked, node_map, axis=3)
    panels = nodes.reshape(N_GX, N_GY * PANELS, NODES)
    low_panels = panels.astype(jnp.bfloat16)

    def one_slab(items):
        low_group, list_group, block_group, panel_group = items
        chosen = low_group[list_group]
        product = jnp.einsum("tkij,tkj->ti", block_group.astype(jnp.float32), chosen.astype(jnp.float32))
        return product - 0.5 * panel_group

    double = lax.map(one_slab, (low_panels, near_list, near_blocks, panels))
    values = double.reshape(N_GX, N_GY, 2, CX * CY)
    index_a = jnp.arange(N_GX, dtype=jnp.int32)[:, None, None, None]
    index_b = jnp.arange(N_GY, dtype=jnp.int32)[None, :, None, None]
    index_c = jnp.arange(2, dtype=jnp.int32)[None, None, :, None]
    cells = jnp.zeros((N_GX, N_GY, 2, CX * CY), jnp.float32).at[index_a, index_b, index_c, node_map].set(values)
    planes = cells.reshape(N_GX, N_GY, 2, CX, CY).transpose(2, 0, 3, 1, 4).reshape(2, NX, NY)
    empty = jnp.zeros((NX, NY), jnp.float32)
    lower = jnp.stack([planes[0], empty])
    upper = jnp.stack([empty, planes[1]])
    extend = reset_planes(jnp.zeros((2, NX, NY, NZ), jnp.float32), lower, upper)
    for sweep in range(EXT_SWEEPS):
        extend = reset_planes(neighbours(extend) / DIAG, lower, upper)
    potential = scalar[0] + extend[0] + extend[1]
    padded = jnp.pad(potential, 1)
    grad_x = (padded[2:, 1:-1, 1:-1] - padded[:-2, 1:-1, 1:-1]) * 0.5
    grad_y = (padded[1:-1, 2:, 1:-1] - padded[1:-1, :-2, 1:-1]) * 0.5
    grad_z = (padded[1:-1, 1:-1, 2:] - padded[1:-1, 1:-1, :-2]) * 0.5
    field = exch_coef[None] * laplace - jnp.stack([grad_x, grad_y, grad_z])
    return field, potential
```

```python
import jax
import jax.numpy as jnp
from jax import lax
from jax.sharding import PartitionSpec as P

NODES = 128
SWEEPS = 8
EXT_SWEEPS = 4
NMAT = 4


SCREEN = 0.25
DIAG = 6.0 + SCREEN


def _pairs(count, step):
    return [(i, i + step) for i in range(count) if 0 <= i + step < count]


def _pack(arrays):
    return jnp.concatenate([a.reshape(-1) for a in arrays])


def _unpack(flat, like):
    out = []
    start = 0
    for a in like:
        out.append(flat[start : start + a.size].reshape(a.shape))
        start += a.size
    return out


def swap(axis, to_next, to_prev):
    count = lax.axis_size(axis)
    if len(to_next) == 1:
        from_prev = [lax.ppermute(to_next[0], axis, _pairs(count, 1))]
        from_next = [lax.ppermute(to_prev[0], axis, _pairs(count, -1))]
        return from_prev, from_next
    from_prev = lax.ppermute(_pack(to_next), axis, _pairs(count, 1))
    from_next = lax.ppermute(_pack(to_prev), axis, _pairs(count, -1))
    return _unpack(from_prev, to_next), _unpack(from_next, to_prev)


def widen(block, hx, hy, dx, dy):
    size_x = block.shape[dx]
    (lo,), (hi,) = swap(
        "gx",
        [lax.slice_in_dim(block, size_x - hx, size_x, axis=dx)],
        [lax.slice_in_dim(block, 0, hx, axis=dx)],
    )
    block = jnp.concatenate([lo, block, hi], axis=dx)
    size_y = block.shape[dy]
    (lo,), (hi,) = swap(
        "gy",
        [lax.slice_in_dim(block, size_y - hy, size_y, axis=dy)],
        [lax.slice_in_dim(block, 0, hy, axis=dy)],
    )
    return jnp.concatenate([lo, block, hi], axis=dy)


def zpad(a):
    return jnp.pad(a, [(0, 0)] * (a.ndim - 1) + [(1, 1)])


def near_sum(wide):
    padded = zpad(wide)
    total = wide[..., 2:, 1:-1, :] + wide[..., :-2, 1:-1, :]
    total = total + wide[..., 1:-1, 2:, :] + wide[..., 1:-1, :-2, :]
    total = total + padded[..., 1:-1, 1:-1, 2:] + padded[..., 1:-1, 1:-1, :-2]
    return total


def lookup(grain_ids, table):
    result = jnp.zeros(grain_ids.shape, jnp.float32)
    for index in range(NMAT):
        result = result + (grain_ids == index).astype(jnp.float32) * table[index]
    return result


def body(magnet, grain_ids, exch_table, sat_table, surface_map, near_list, near_blocks):
    cells_x = magnet.shape[1]
    cells_y = magnet.shape[2]
    cells_z = magnet.shape[3]
    grid_x = cells_x * lax.axis_size("gx")
    grid_y = cells_y * lax.axis_size("gy")
    base_x = lax.axis_index("gx") * cells_x
    base_y = lax.axis_index("gy") * cells_y

    def inside(h):
        xs = base_x - h + jnp.arange(cells_x + 2 * h, dtype=jnp.int32)
        ys = base_y - h + jnp.arange(cells_y + 2 * h, dtype=jnp.int32)
        ok_x = (xs >= 0) & (xs < grid_x)
        ok_y = (ys >= 0) & (ys < grid_y)
        return (ok_x[:, None] & ok_y[None, :])[:, :, None]

    exch_coef = lookup(grain_ids, exch_table)
    sat_coef = lookup(grain_ids, sat_table)

    halo = SWEEPS
    data = jnp.concatenate([magnet, sat_coef[None]], axis=0)
    wide = widen(data, halo, halo, 1, 2)
    m0, m1, m2, sat_w = wide[0], wide[1], wide[2], wide[3]

    hs = halo - 1
    ex = slice(1, 1 + cells_x + 2 * hs)
    ey = slice(1, 1 + cells_y + 2 * hs)
    m2p = zpad(m2[ex, ey])
    diverge = (
        m0[2 : 2 + cells_x + 2 * hs, ey]
        - m0[0 : cells_x + 2 * hs, ey]
        + m1[ex, 2 : 2 + cells_y + 2 * hs]
        - m1[ex, 0 : cells_y + 2 * hs]
        + m2p[:, :, 2:]
        - m2p[:, :, :-2]
    ) * 0.5
    source = -sat_w[ex, ey] * diverge

    scalar = jnp.where(inside(hs), source / DIAG, 0.0)
    for sweep in range(1, SWEEPS):
        h = hs - sweep
        off = hs - h
        src = source[off : off + cells_x + 2 * h, off : off + cells_y + 2 * h]
        value = (near_sum(scalar) + src) / DIAG
        scalar = jnp.where(inside(h), value, 0.0) if h > 0 else value

    mag_1 = wide[0:3, halo - 1 : halo + 1 + cells_x, halo - 1 : halo + 1 + cells_y]
    laplace = near_sum(mag_1) - 6.0 * magnet

    node_map = surface_map[:, 0, :]
    cell_ids = jnp.arange(cells_x * cells_y, dtype=jnp.int32)
    onehot = node_map[:, :, None] == cell_ids[None, None, :]
    face_vals = jnp.stack([scalar[:, :, 0], scalar[:, :, -1]]).reshape(2, cells_x * cells_y)
    panels = jnp.sum(jnp.where(onehot, face_vals[:, None, :], 0.0), axis=2)
    low_panels = panels.astype(jnp.bfloat16)
    local_list = near_list[0]
    blank_pick = jnp.zeros((local_list.shape[0], local_list.shape[1], NODES), jnp.bfloat16)
    piece = lax.all_gather(low_panels, "gy", axis=0, tiled=True)
    valid = (local_list >= 0) & (local_list < piece.shape[0])
    picked = piece[jnp.clip(local_list, 0, piece.shape[0] - 1)]
    chosen = jnp.where(valid[:, :, None], picked, blank_pick)
    double = (
        jnp.einsum("tkij,tkj->ti", near_blocks[0], chosen, preferred_element_type=jnp.float32)
        - 0.5 * panels
    )
    cells = jnp.sum(jnp.where(onehot, double[:, :, None], 0.0), axis=1)
    planes = cells.reshape(2, cells_x, cells_y)

    he = EXT_SWEEPS + 1
    (p_lo, s_lo), (p_hi, s_hi) = swap(
        "gx",
        [planes[:, cells_x - he :], scalar[cells_x - 1 :]],
        [planes[:, :he], scalar[:1]],
    )
    planes_x = jnp.concatenate([p_lo, planes, p_hi], axis=1)
    (q_lo, t_lo), (q_hi, t_hi) = swap(
        "gy",
        [planes_x[:, :, cells_y - he :], scalar[:, cells_y - 1 :]],
        [planes_x[:, :, :he], scalar[:, :1]],
    )
    planes_w = jnp.concatenate([q_lo, planes_x, q_hi], axis=2)

    column = jnp.concatenate([s_lo, scalar, s_hi], axis=0)
    row_pad = ((1, 1), (0, 0), (0, 0))
    scalar_1 = jnp.concatenate([jnp.pad(t_lo, row_pad), column, jnp.pad(t_hi, row_pad)], axis=1)

    z_ids = jnp.arange(cells_z, dtype=jnp.int32)
    bottom = z_ids == 0
    top = z_ids == cells_z - 1
    zero_w = jnp.zeros_like(planes_w[0])

    def reset(values, off, size_x, size_y):
        sub = planes_w[:, off : off + size_x, off : off + size_y]
        zero = zero_w[off : off + size_x, off : off + size_y]
        lower = jnp.stack([sub[0], zero])[..., None]
        upper = jnp.stack([zero, sub[1]])[..., None]
        return jnp.where(bottom, lower, jnp.where(top, upper, values))

    extend = reset(
        jnp.zeros((2,) + planes_w.shape[1:] + (cells_z,), jnp.float32),
        0,
        planes_w.shape[1],
        planes_w.shape[2],
    )
    for sweep in range(EXT_SWEEPS):
        h = he - 1 - sweep
        off = he - h
        value = jnp.where(inside(h), near_sum(extend) / DIAG, 0.0)
        extend = reset(value, off, cells_x + 2 * h, cells_y + 2 * h)

    potential_1 = scalar_1 + extend[0] + extend[1]
    potential = potential_1[1:-1, 1:-1]
    padded = zpad(potential_1)
    grad_x = (potential_1[2:, 1:-1] - potential_1[:-2, 1:-1]) * 0.5
    grad_y = (potential_1[1:-1, 2:] - potential_1[1:-1, :-2]) * 0.5
    grad_z = (padded[1:-1, 1:-1, 2:] - padded[1:-1, 1:-1, :-2]) * 0.5
    field = exch_coef[None] * laplace - jnp.stack([grad_x, grad_y, grad_z])
    return (field, potential)


def solution(mesh):
    return jax.shard_map(
        body,
        mesh=mesh,
        in_specs=(
            P(None, "gx", "gy", None),
            P("gx", "gy", None),
            P(),
            P(),
            P("gx", "gy", None),
            P("gx", "gy", None),
            P("gx", "gy", None, None, None),
        ),
        out_specs=(P(None, "gx", "gy", None), P("gx", "gy", None)),
        check_vma=False,
    )
```

```python
import jax
import jax.numpy as jnp
from jax import lax
from jax.sharding import PartitionSpec as P

NODES = 128
SWEEPS = 8
EXT_SWEEPS = 4
NMAT = 4


SCREEN = 0.25
DIAG = 6.0 + SCREEN


def _pairs(count, step):
    return [(i, i + step) for i in range(count) if 0 <= i + step < count]


def _pack(arrays):
    return jnp.concatenate([a.reshape(-1) for a in arrays])


def _unpack(flat, like):
    out = []
    start = 0
    for a in like:
        out.append(flat[start : start + a.size].reshape(a.shape))
        start += a.size
    return out


def swap(axis, to_next, to_prev):
    count = lax.axis_size(axis)
    if len(to_next) == 1:
        from_prev = [lax.ppermute(to_next[0], axis, _pairs(count, 1))]
        from_next = [lax.ppermute(to_prev[0], axis, _pairs(count, -1))]
        return from_prev, from_next
    from_prev = lax.ppermute(_pack(to_next), axis, _pairs(count, 1))
    from_next = lax.ppermute(_pack(to_prev), axis, _pairs(count, -1))
    return _unpack(from_prev, to_next), _unpack(from_next, to_prev)


def widen(block, hx, hy, dx, dy):
    size_x = block.shape[dx]
    (lo,), (hi,) = swap(
        "gx",
        [lax.slice_in_dim(block, size_x - hx, size_x, axis=dx)],
        [lax.slice_in_dim(block, 0, hx, axis=dx)],
    )
    block = jnp.concatenate([lo, block, hi], axis=dx)
    size_y = block.shape[dy]
    (lo,), (hi,) = swap(
        "gy",
        [lax.slice_in_dim(block, size_y - hy, size_y, axis=dy)],
        [lax.slice_in_dim(block, 0, hy, axis=dy)],
    )
    return jnp.concatenate([lo, block, hi], axis=dy)


def zpad(a):
    return jnp.pad(a, [(0, 0)] * (a.ndim - 1) + [(1, 1)])


def near_sum(wide):
    padded = zpad(wide)
    total = wide[..., 2:, 1:-1, :] + wide[..., :-2, 1:-1, :]
    total = total + wide[..., 1:-1, 2:, :] + wide[..., 1:-1, :-2, :]
    total = total + padded[..., 1:-1, 1:-1, 2:] + padded[..., 1:-1, 1:-1, :-2]
    return total


def lookup(grain_ids, table):
    result = jnp.zeros(grain_ids.shape, jnp.float32)
    for index in range(NMAT):
        result = result + (grain_ids == index).astype(jnp.float32) * table[index]
    return result


def body(magnet, grain_ids, exch_table, sat_table, surface_map, near_list, near_blocks):
    cells_x = magnet.shape[1]
    cells_y = magnet.shape[2]
    cells_z = magnet.shape[3]
    grid_x = cells_x * lax.axis_size("gx")
    grid_y = cells_y * lax.axis_size("gy")
    base_x = lax.axis_index("gx") * cells_x
    base_y = lax.axis_index("gy") * cells_y

    def inside(h):
        xs = base_x - h + jnp.arange(cells_x + 2 * h, dtype=jnp.int32)
        ys = base_y - h + jnp.arange(cells_y + 2 * h, dtype=jnp.int32)
        ok_x = (xs >= 0) & (xs < grid_x)
        ok_y = (ys >= 0) & (ys < grid_y)
        return (ok_x[:, None] & ok_y[None, :])[:, :, None]

    halo = SWEEPS
    data = jnp.concatenate([magnet, grain_ids.astype(jnp.float32)[None]], axis=0)
    wide = widen(data, halo, halo, 1, 2)
    m0, m1, m2 = wide[0], wide[1], wide[2]
    exch_coef = lookup(grain_ids, exch_table)

    hs = halo - 1
    ex = slice(1, 1 + cells_x + 2 * hs)
    ey = slice(1, 1 + cells_y + 2 * hs)
    m2p = zpad(m2[ex, ey])
    diverge = (
        m0[2 : 2 + cells_x + 2 * hs, ey]
        - m0[0 : cells_x + 2 * hs, ey]
        + m1[ex, 2 : 2 + cells_y + 2 * hs]
        - m1[ex, 0 : cells_y + 2 * hs]
        + m2p[:, :, 2:]
        - m2p[:, :, :-2]
    ) * 0.5
    sat_w = lookup(wide[3, ex, ey].astype(jnp.int32), sat_table)
    source = -sat_w * diverge

    scalar = jnp.where(inside(hs), source / DIAG, 0.0)
    for sweep in range(1, SWEEPS):
        h = hs - sweep
        off = hs - h
        src = source[off : off + cells_x + 2 * h, off : off + cells_y + 2 * h]
        value = (near_sum(scalar) + src) / DIAG
        scalar = jnp.where(inside(h), value, 0.0) if h > 0 else value

    mag_1 = wide[0:3, halo - 1 : halo + 1 + cells_x, halo - 1 : halo + 1 + cells_y]
    laplace = near_sum(mag_1) - 6.0 * magnet

    node_map = surface_map[:, 0, :]
    cell_ids = jnp.arange(cells_x * cells_y, dtype=jnp.int32)
    onehot = node_map[:, :, None] == cell_ids[None, None, :]
    face_vals = jnp.stack([scalar[:, :, 0], scalar[:, :, -1]]).reshape(2, cells_x * cells_y)
    panels = jnp.sum(jnp.where(onehot, face_vals[:, None, :], 0.0), axis=2)
    low_panels = panels.astype(jnp.bfloat16)
    local_list = near_list[0]
    blank_pick = jnp.zeros((local_list.shape[0], local_list.shape[1], NODES), jnp.bfloat16)
    group = lax.axis_size("gy")
    copies = jnp.broadcast_to(low_panels[None], (group,) + low_panels.shape)
    piece = lax.all_to_all(copies, "gy", 0, 0, tiled=True).reshape(group * 2, NODES)
    valid = (local_list >= 0) & (local_list < piece.shape[0])
    picked = piece[jnp.clip(local_list, 0, piece.shape[0] - 1)]
    chosen = jnp.where(valid[:, :, None], picked, blank_pick)
    double = (
        jnp.einsum("tkij,tkj->ti", near_blocks[0], chosen, preferred_element_type=jnp.float32)
        - 0.5 * panels
    )
    cells = jnp.sum(jnp.where(onehot, double[:, :, None], 0.0), axis=1)
    planes = cells.reshape(2, cells_x, cells_y)

    he = EXT_SWEEPS + 1
    (p_lo, s_lo), (p_hi, s_hi) = swap(
        "gx",
        [planes[:, cells_x - he :], scalar[cells_x - 1 :]],
        [planes[:, :he], scalar[:1]],
    )
    planes_x = jnp.concatenate([p_lo, planes, p_hi], axis=1)
    (q_lo, t_lo), (q_hi, t_hi) = swap(
        "gy",
        [planes_x[:, :, cells_y - he :], scalar[:, cells_y - 1 :]],
        [planes_x[:, :, :he], scalar[:, :1]],
    )
    planes_w = jnp.concatenate([q_lo, planes_x, q_hi], axis=2)

    column = jnp.concatenate([s_lo, scalar, s_hi], axis=0)
    row_pad = ((1, 1), (0, 0), (0, 0))
    scalar_1 = jnp.concatenate([jnp.pad(t_lo, row_pad), column, jnp.pad(t_hi, row_pad)], axis=1)

    z_ids = jnp.arange(cells_z, dtype=jnp.int32)
    bottom = z_ids == 0
    top = z_ids == cells_z - 1
    zero_w = jnp.zeros_like(planes_w[0])

    def reset(values, off, size_x, size_y):
        sub = planes_w[:, off : off + size_x, off : off + size_y]
        zero = zero_w[off : off + size_x, off : off + size_y]
        lower = jnp.stack([sub[0], zero])[..., None]
        upper = jnp.stack([zero, sub[1]])[..., None]
        return jnp.where(bottom, lower, jnp.where(top, upper, values))

    extend = reset(
        jnp.zeros((2,) + planes_w.shape[1:] + (cells_z,), jnp.float32),
        0,
        planes_w.shape[1],
        planes_w.shape[2],
    )
    for sweep in range(EXT_SWEEPS):
        h = he - 1 - sweep
        off = he - h
        value = jnp.where(inside(h), near_sum(extend) / DIAG, 0.0)
        extend = reset(value, off, cells_x + 2 * h, cells_y + 2 * h)

    potential_1 = scalar_1 + extend[0] + extend[1]
    potential = potential_1[1:-1, 1:-1]
    padded = zpad(potential_1)
    grad_x = (potential_1[2:, 1:-1] - potential_1[:-2, 1:-1]) * 0.5
    grad_y = (potential_1[1:-1, 2:] - potential_1[1:-1, :-2]) * 0.5
    grad_z = (padded[1:-1, 1:-1, 2:] - padded[1:-1, 1:-1, :-2]) * 0.5
    field = exch_coef[None] * laplace - jnp.stack([grad_x, grad_y, grad_z])
    return (field, potential)


def solution(mesh):
    return jax.shard_map(
        body,
        mesh=mesh,
        in_specs=(
            P(None, "gx", "gy", None),
            P("gx", "gy", None),
            P(),
            P(),
            P("gx", "gy", None),
            P("gx", "gy", None),
            P("gx", "gy", None, None, None),
        ),
        out_specs=(P(None, "gx", "gy", None), P("gx", "gy", None)),
        check_vma=False,
    )
```

```python
import jax
import jax.numpy as jnp
from jax import lax
from jax.sharding import PartitionSpec as P


NODES = 128
SWEEPS = 8
EXT_SWEEPS = 4
NMAT = 4


SCREEN = 0.25
DIAG = 6.0 + SCREEN


def _pairs(count, step):
    return [(i, i + step) for i in range(count) if 0 <= i + step < count]


def _pack(arrays):
    return jnp.concatenate([a.reshape(-1) for a in arrays])


def _unpack(flat, like):
    out = []
    start = 0
    for a in like:
        out.append(flat[start : start + a.size].reshape(a.shape))
        start += a.size
    return out


def swap(axis, to_next, to_prev):
    count = lax.axis_size(axis)
    if len(to_next) == 1:
        from_prev = [lax.ppermute(to_next[0], axis, _pairs(count, 1))]
        from_next = [lax.ppermute(to_prev[0], axis, _pairs(count, -1))]
        return from_prev, from_next
    from_prev = lax.ppermute(_pack(to_next), axis, _pairs(count, 1))
    from_next = lax.ppermute(_pack(to_prev), axis, _pairs(count, -1))
    return _unpack(from_prev, to_next), _unpack(from_next, to_prev)


def _diag_pairs(count_x, count_y, step_x, step_y):
    return [
        (i * count_y + j, (i + step_x) * count_y + j + step_y)
        for i in range(count_x)
        for j in range(count_y)
        if 0 <= i + step_x < count_x and 0 <= j + step_y < count_y
    ]


def widen(block, hx, hy, dx, dy, ride_x=(), ride_y=()):
    size_x = block.shape[dx]
    size_y = block.shape[dy]
    count_x = lax.axis_size("gx")
    count_y = lax.axis_size("gy")
    part_x = {1: (size_x - hx, size_x), -1: (0, hx)}
    part_y = {1: (size_y - hy, size_y), -1: (0, hy)}
    corner = {}
    for step_x in (1, -1):
        for step_y in (1, -1):
            piece = lax.slice_in_dim(block, *part_x[step_x], axis=dx)
            piece = lax.slice_in_dim(piece, *part_y[step_y], axis=dy)
            corner[(step_x, step_y)] = lax.ppermute(
                piece, ("gx", "gy"), _diag_pairs(count_x, count_y, step_x, step_y)
            )
    (lo_x, *got_lo_x), (hi_x, *got_hi_x) = swap(
        "gx",
        [lax.slice_in_dim(block, *part_x[1], axis=dx)] + [r[0] for r in ride_x],
        [lax.slice_in_dim(block, *part_x[-1], axis=dx)] + [r[1] for r in ride_x],
    )
    (lo_y, *got_lo_y), (hi_y, *got_hi_y) = swap(
        "gy",
        [lax.slice_in_dim(block, *part_y[1], axis=dy)] + [r[0] for r in ride_y],
        [lax.slice_in_dim(block, *part_y[-1], axis=dy)] + [r[1] for r in ride_y],
    )
    low = jnp.concatenate([corner[(1, 1)], lo_x, corner[(1, -1)]], axis=dy)
    mid = jnp.concatenate([lo_y, block, hi_y], axis=dy)
    high = jnp.concatenate([corner[(-1, 1)], hi_x, corner[(-1, -1)]], axis=dy)
    wide = jnp.concatenate([low, mid, high], axis=dx)
    return wide, (got_lo_x, got_hi_x), (got_lo_y, got_hi_y)


def zpad(a):
    return jnp.pad(a, [(0, 0)] * (a.ndim - 1) + [(1, 1)])


def near_sum(wide):
    padded = zpad(wide)
    total = wide[..., 2:, 1:-1, :] + wide[..., :-2, 1:-1, :]
    total = total + wide[..., 1:-1, 2:, :] + wide[..., 1:-1, :-2, :]
    total = total + padded[..., 1:-1, 1:-1, 2:] + padded[..., 1:-1, 1:-1, :-2]
    return total


def lookup(grain_ids, table):
    result = jnp.zeros(grain_ids.shape, jnp.float32)
    for index in range(NMAT):
        result = result + (grain_ids == index).astype(jnp.float32) * table[index]
    return result


def body(magnet, grain_ids, exch_table, sat_table, surface_map, near_list, near_blocks):
    cells_x = magnet.shape[1]
    cells_y = magnet.shape[2]
    cells_z = magnet.shape[3]
    grid_x = cells_x * lax.axis_size("gx")
    grid_y = cells_y * lax.axis_size("gy")
    base_x = lax.axis_index("gx") * cells_x
    base_y = lax.axis_index("gy") * cells_y

    def inside(h):
        xs = base_x - h + jnp.arange(cells_x + 2 * h, dtype=jnp.int32)
        ys = base_y - h + jnp.arange(cells_y + 2 * h, dtype=jnp.int32)
        ok_x = (xs >= 0) & (xs < grid_x)
        ok_y = (ys >= 0) & (ys < grid_y)
        return (ok_x[:, None] & ok_y[None, :])[:, :, None]

    halo = SWEEPS
    data = jnp.concatenate([magnet, grain_ids.astype(jnp.float32)[None]], axis=0)
    wide, _, _ = widen(data, halo, halo, 1, 2)
    m0, m1, m2 = wide[0], wide[1], wide[2]
    exch_coef = lookup(grain_ids, exch_table)

    hs = halo - 1
    ex = slice(1, 1 + cells_x + 2 * hs)
    ey = slice(1, 1 + cells_y + 2 * hs)
    m2p = zpad(m2[ex, ey])
    diverge = (
        m0[2 : 2 + cells_x + 2 * hs, ey]
        - m0[0 : cells_x + 2 * hs, ey]
        + m1[ex, 2 : 2 + cells_y + 2 * hs]
        - m1[ex, 0 : cells_y + 2 * hs]
        + m2p[:, :, 2:]
        - m2p[:, :, :-2]
    ) * 0.5
    sat_w = lookup(wide[3, ex, ey].astype(jnp.int32), sat_table)
    source = -sat_w * diverge

    scalar = jnp.where(inside(hs), source / DIAG, 0.0)
    for sweep in range(1, SWEEPS):
        h = hs - sweep
        off = hs - h
        src = source[off : off + cells_x + 2 * h, off : off + cells_y + 2 * h]
        value = (near_sum(scalar) + src) / DIAG
        scalar = jnp.where(inside(h), value, 0.0) if h > 0 else value

    mag_1 = wide[0:3, halo - 1 : halo + 1 + cells_x, halo - 1 : halo + 1 + cells_y]
    laplace = near_sum(mag_1) - 6.0 * magnet

    node_map = surface_map[:, 0, :]
    cell_ids = jnp.arange(cells_x * cells_y, dtype=jnp.int32)
    onehot = node_map[:, :, None] == cell_ids[None, None, :]
    face_vals = jnp.stack([scalar[:, :, 0], scalar[:, :, -1]]).reshape(2, cells_x * cells_y)
    panels = jnp.sum(jnp.where(onehot, face_vals[:, None, :], 0.0), axis=2)
    low_panels = panels.astype(jnp.bfloat16)
    local_list = near_list[0]
    blank_pick = jnp.zeros((local_list.shape[0], local_list.shape[1], NODES), jnp.bfloat16)
    group = lax.axis_size("gy")
    copies = jnp.broadcast_to(low_panels[None], (group,) + low_panels.shape)
    piece = lax.all_to_all(copies, "gy", 0, 0, tiled=True).reshape(group * 2, NODES)
    valid = (local_list >= 0) & (local_list < piece.shape[0])
    picked = piece[jnp.clip(local_list, 0, piece.shape[0] - 1)]
    chosen = jnp.where(valid[:, :, None], picked, blank_pick)
    double = (
        jnp.einsum("tkij,tkj->ti", near_blocks[0], chosen, preferred_element_type=jnp.float32)
        - 0.5 * panels
    )
    cells = jnp.sum(jnp.where(onehot, double[:, :, None], 0.0), axis=1)
    planes = cells.reshape(2, cells_x, cells_y)

    he = EXT_SWEEPS + 1
    planes_w, ((s_lo,), (s_hi,)), ((t_lo,), (t_hi,)) = widen(
        planes,
        he,
        he,
        1,
        2,
        ride_x=[(scalar[cells_x - 1 :], scalar[:1])],
        ride_y=[(scalar[:, cells_y - 1 :], scalar[:, :1])],
    )

    column = jnp.concatenate([s_lo, scalar, s_hi], axis=0)
    row_pad = ((1, 1), (0, 0), (0, 0))
    scalar_1 = jnp.concatenate([jnp.pad(t_lo, row_pad), column, jnp.pad(t_hi, row_pad)], axis=1)

    z_ids = jnp.arange(cells_z, dtype=jnp.int32)
    bottom = z_ids == 0
    top = z_ids == cells_z - 1
    zero_w = jnp.zeros_like(planes_w[0])

    def reset(values, off, size_x, size_y):
        sub = planes_w[:, off : off + size_x, off : off + size_y]
        zero = zero_w[off : off + size_x, off : off + size_y]
        lower = jnp.stack([sub[0], zero])[..., None]
        upper = jnp.stack([zero, sub[1]])[..., None]
        return jnp.where(bottom, lower, jnp.where(top, upper, values))

    extend = reset(
        jnp.zeros((2,) + planes_w.shape[1:] + (cells_z,), jnp.float32),
        0,
        planes_w.shape[1],
        planes_w.shape[2],
    )
    for sweep in range(EXT_SWEEPS):
        h = he - 1 - sweep
        off = he - h
        value = jnp.where(inside(h), near_sum(extend) / DIAG, 0.0)
        extend = reset(value, off, cells_x + 2 * h, cells_y + 2 * h)

    potential_1 = scalar_1 + extend[0] + extend[1]
    potential = potential_1[1:-1, 1:-1]
    padded = zpad(potential_1)
    grad_x = (potential_1[2:, 1:-1] - potential_1[:-2, 1:-1]) * 0.5
    grad_y = (potential_1[1:-1, 2:] - potential_1[1:-1, :-2]) * 0.5
    grad_z = (padded[1:-1, 1:-1, 2:] - padded[1:-1, 1:-1, :-2]) * 0.5
    field = exch_coef[None] * laplace - jnp.stack([grad_x, grad_y, grad_z])
    return (field, potential)


def solution(mesh):
    return jax.shard_map(
        body,
        mesh=mesh,
        in_specs=(
            P(None, "gx", "gy", None),
            P("gx", "gy", None),
            P(),
            P(),
            P("gx", "gy", None),
            P("gx", "gy", None),
            P("gx", "gy", None, None, None),
        ),
        out_specs=(P(None, "gx", "gy", None), P("gx", "gy", None)),
        check_vma=False,
    )
```

```python
import jax
import jax.numpy as jnp
from jax import lax
from jax.sharding import PartitionSpec as P

NODES = 128
SWEEPS = 8
EXT_SWEEPS = 4
NMAT = 4


SCREEN = 0.25
DIAG = 6.0 + SCREEN


def _pairs(count, step):
    return [(i, i + step) for i in range(count) if 0 <= i + step < count]


def _pack(arrays):
    return jnp.concatenate([a.reshape(-1) for a in arrays])


def _unpack(flat, like):
    out = []
    start = 0
    for a in like:
        out.append(flat[start : start + a.size].reshape(a.shape))
        start += a.size
    return out


def swap(axis, to_next, to_prev):
    count = lax.axis_size(axis)
    if len(to_next) == 1:
        from_prev = [lax.ppermute(to_next[0], axis, _pairs(count, 1))]
        from_next = [lax.ppermute(to_prev[0], axis, _pairs(count, -1))]
        return from_prev, from_next
    from_prev = lax.ppermute(_pack(to_next), axis, _pairs(count, 1))
    from_next = lax.ppermute(_pack(to_prev), axis, _pairs(count, -1))
    return _unpack(from_prev, to_next), _unpack(from_next, to_prev)


def widen(block, hx, hy, dx, dy):
    size_x = block.shape[dx]
    (lo,), (hi,) = swap(
        "gx",
        [lax.slice_in_dim(block, size_x - hx, size_x, axis=dx)],
        [lax.slice_in_dim(block, 0, hx, axis=dx)],
    )
    block = jnp.concatenate([lo, block, hi], axis=dx)
    size_y = block.shape[dy]
    (lo,), (hi,) = swap(
        "gy",
        [lax.slice_in_dim(block, size_y - hy, size_y, axis=dy)],
        [lax.slice_in_dim(block, 0, hy, axis=dy)],
    )
    return jnp.concatenate([lo, block, hi], axis=dy)


def zpad(a):
    return jnp.pad(a, [(0, 0)] * (a.ndim - 1) + [(1, 1)])


def near_sum(wide):
    padded = zpad(wide)
    total = wide[..., 2:, 1:-1, :] + wide[..., :-2, 1:-1, :]
    total = total + wide[..., 1:-1, 2:, :] + wide[..., 1:-1, :-2, :]
    total = total + padded[..., 1:-1, 1:-1, 2:] + padded[..., 1:-1, 1:-1, :-2]
    return total


def lookup(grain_ids, table):
    result = jnp.zeros(grain_ids.shape, jnp.float32)
    for index in range(NMAT):
        result = result + (grain_ids == index).astype(jnp.float32) * table[index]
    return result


def body(magnet, grain_ids, exch_table, sat_table, surface_map, near_list, near_blocks):
    cells_x = magnet.shape[1]
    cells_y = magnet.shape[2]
    cells_z = magnet.shape[3]
    grid_x = cells_x * lax.axis_size("gx")
    grid_y = cells_y * lax.axis_size("gy")
    base_x = lax.axis_index("gx") * cells_x
    base_y = lax.axis_index("gy") * cells_y

    def inside(h):
        xs = base_x - h + jnp.arange(cells_x + 2 * h, dtype=jnp.int32)
        ys = base_y - h + jnp.arange(cells_y + 2 * h, dtype=jnp.int32)
        ok_x = (xs >= 0) & (xs < grid_x)
        ok_y = (ys >= 0) & (ys < grid_y)
        return (ok_x[:, None] & ok_y[None, :])[:, :, None]

    halo = SWEEPS
    he = EXT_SWEEPS + 1
    node_map = surface_map[:, 0, :]
    cell_ids = jnp.arange(cells_x * cells_y, dtype=jnp.int32)
    onehot = node_map[:, :, None] == cell_ids[None, None, :]
    rows = jnp.einsum(
        "tnc,tknj->tkcj",
        onehot.astype(near_blocks.dtype),
        near_blocks[0],
        preferred_element_type=jnp.float32,
    )
    rows = rows.reshape(rows.shape[0], rows.shape[1], cells_x, cells_y, NODES)
    local_list = near_list[0]
    list_f = local_list.astype(jnp.float32)

    data = jnp.concatenate([magnet, grain_ids.astype(jnp.float32)[None]], axis=0)
    (lo,), (hi,) = swap("gx", [data[:, cells_x - halo :]], [data[:, :halo]])
    wide_x = jnp.concatenate([lo, data, hi], axis=1)
    (lo, rows_lo, list_lo), (hi, rows_hi, list_hi) = swap(
        "gy",
        [wide_x[:, :, cells_y - halo :], rows[:, :, :, cells_y - he :], list_f],
        [wide_x[:, :, :halo], rows[:, :, :, :he], list_f],
    )
    wide = jnp.concatenate([lo, wide_x, hi], axis=2)
    m0, m1, m2 = wide[0], wide[1], wide[2]
    exch_coef = lookup(grain_ids, exch_table)

    hs = halo - 1
    ex = slice(1, 1 + cells_x + 2 * hs)
    ey = slice(1, 1 + cells_y + 2 * hs)
    m2p = zpad(m2[ex, ey])
    diverge = (
        m0[2 : 2 + cells_x + 2 * hs, ey]
        - m0[0 : cells_x + 2 * hs, ey]
        + m1[ex, 2 : 2 + cells_y + 2 * hs]
        - m1[ex, 0 : cells_y + 2 * hs]
        + m2p[:, :, 2:]
        - m2p[:, :, :-2]
    ) * 0.5
    sat_w = lookup(wide[3, ex, ey].astype(jnp.int32), sat_table)
    source = -sat_w * diverge

    scalar = jnp.where(inside(hs), source / DIAG, 0.0)
    for sweep in range(1, SWEEPS):
        h = hs - sweep
        off = hs - h
        src = source[off : off + cells_x + 2 * h, off : off + cells_y + 2 * h]
        value = (near_sum(scalar) + src) / DIAG
        scalar = jnp.where(inside(h), value, 0.0) if h > 0 else value

    mag_1 = wide[0:3, halo - 1 : halo + 1 + cells_x, halo - 1 : halo + 1 + cells_y]
    laplace = near_sum(mag_1) - 6.0 * magnet

    face = jnp.stack([scalar[:, :, 0], scalar[:, :, -1]])
    face_flat = face.reshape(2, cells_x * cells_y)
    panels = jnp.sum(jnp.where(onehot, face_flat[:, None, :], 0.0), axis=2)

    group = lax.axis_size("gy")
    me = lax.axis_index("gy")
    side_hi = _pack([face[:, :, cells_y - he :], scalar[:, cells_y - 1]])
    side_lo = _pack([face[:, :, :he], scalar[:, 0]])
    rel = jnp.arange(group, dtype=jnp.int32)[:, None] - me
    side = jnp.where(rel == 1, side_hi[None], jnp.where(rel == -1, side_lo[None], 0.0))
    chunks = jnp.concatenate(
        [jnp.broadcast_to(panels.reshape(1, -1), (group, panels.size)), side], axis=1
    )
    got = lax.all_to_all(chunks, "gy", 0, 0, tiled=True)
    piece = got[:, : panels.size].reshape(group * 2, NODES).astype(jnp.bfloat16)
    from_lo = jnp.where(me > 0, got[jnp.maximum(me - 1, 0), panels.size :], 0.0)
    from_hi = jnp.where(me < group - 1, got[jnp.minimum(me + 1, group - 1), panels.size :], 0.0)
    like = [face[:, :, :he], scalar[:, 0]]
    face_lo, t_lo = _unpack(from_lo, like)
    face_hi, t_hi = _unpack(from_hi, like)

    def double_of(block_rows, lists, faces):
        lists = lists.astype(jnp.int32)
        valid = (lists >= 0) & (lists < piece.shape[0])
        picked = piece[jnp.clip(lists, 0, piece.shape[0] - 1)]
        chosen = jnp.where(valid[:, :, None], picked, jnp.zeros_like(picked))
        product = jnp.einsum(
            "tkxyj,tkj->txy",
            block_rows.astype(jnp.bfloat16),
            chosen,
            preferred_element_type=jnp.float32,
        )
        return product - 0.5 * faces

    planes_y = jnp.concatenate(
        [
            double_of(rows_lo, list_lo, face_lo),
            double_of(rows, local_list, face),
            double_of(rows_hi, list_hi, face_hi),
        ],
        axis=2,
    )

    (p_lo, s_lo), (p_hi, s_hi) = swap(
        "gx",
        [planes_y[:, cells_x - he :], scalar[cells_x - 1 :]],
        [planes_y[:, :he], scalar[:1]],
    )
    planes_w = jnp.concatenate([p_lo, planes_y, p_hi], axis=1)

    column = jnp.concatenate([s_lo, scalar, s_hi], axis=0)
    row_pad = ((1, 1), (0, 0), (0, 0))
    t_lo = jnp.pad(t_lo[:, None], row_pad)
    t_hi = jnp.pad(t_hi[:, None], row_pad)
    scalar_1 = jnp.concatenate([t_lo, column, t_hi], axis=1)

    z_ids = jnp.arange(cells_z, dtype=jnp.int32)
    bottom = z_ids == 0
    top = z_ids == cells_z - 1
    zero_w = jnp.zeros_like(planes_w[0])

    def reset(values, off, size_x, size_y):
        sub = planes_w[:, off : off + size_x, off : off + size_y]
        zero = zero_w[off : off + size_x, off : off + size_y]
        lower = jnp.stack([sub[0], zero])[..., None]
        upper = jnp.stack([zero, sub[1]])[..., None]
        return jnp.where(bottom, lower, jnp.where(top, upper, values))

    extend = reset(
        jnp.zeros((2,) + planes_w.shape[1:] + (cells_z,), jnp.float32),
        0,
        planes_w.shape[1],
        planes_w.shape[2],
    )
    for sweep in range(EXT_SWEEPS):
        h = he - 1 - sweep
        off = he - h
        value = jnp.where(inside(h), near_sum(extend) / DIAG, 0.0)
        extend = reset(value, off, cells_x + 2 * h, cells_y + 2 * h)

    potential_1 = scalar_1 + extend[0] + extend[1]
    potential = potential_1[1:-1, 1:-1]
    padded = zpad(potential_1)
    grad_x = (potential_1[2:, 1:-1] - potential_1[:-2, 1:-1]) * 0.5
    grad_y = (potential_1[1:-1, 2:] - potential_1[1:-1, :-2]) * 0.5
    grad_z = (padded[1:-1, 1:-1, 2:] - padded[1:-1, 1:-1, :-2]) * 0.5
    field = exch_coef[None] * laplace - jnp.stack([grad_x, grad_y, grad_z])
    return (field, potential)


def solution(mesh):
    return jax.shard_map(
        body,
        mesh=mesh,
        in_specs=(
            P(None, "gx", "gy", None),
            P("gx", "gy", None),
            P(),
            P(),
            P("gx", "gy", None),
            P("gx", "gy", None),
            P("gx", "gy", None, None, None),
        ),
        out_specs=(P(None, "gx", "gy", None), P("gx", "gy", None)),
        check_vma=False,
    )
```

```python
import jax
import jax.numpy as jnp
from jax import lax
from jax.sharding import PartitionSpec as P

NODES = 128
SWEEPS = 8
EXT_SWEEPS = 4
NMAT = 4


SCREEN = 0.25
DIAG = 6.0 + SCREEN


def _pairs(count, step):
    return [(i, i + step) for i in range(count) if 0 <= i + step < count]


def _pack(arrays):
    return jnp.concatenate([a.reshape(-1) for a in arrays])


def _unpack(flat, like):
    out = []
    start = 0
    for a in like:
        out.append(flat[start : start + a.size].reshape(a.shape))
        start += a.size
    return out


def swap(axis, to_next, to_prev):
    count = lax.axis_size(axis)
    if len(to_next) == 1:
        from_prev = [lax.ppermute(to_next[0], axis, _pairs(count, 1))]
        from_next = [lax.ppermute(to_prev[0], axis, _pairs(count, -1))]
        return from_prev, from_next
    from_prev = lax.ppermute(_pack(to_next), axis, _pairs(count, 1))
    from_next = lax.ppermute(_pack(to_prev), axis, _pairs(count, -1))
    return _unpack(from_prev, to_next), _unpack(from_next, to_prev)


def widen(block, hx, hy, dx, dy):
    size_y = block.shape[dy]
    (lo,), (hi,) = swap(
        "gy",
        [lax.slice_in_dim(block, size_y - hy, size_y, axis=dy)],
        [lax.slice_in_dim(block, 0, hy, axis=dy)],
    )
    block = jnp.concatenate([lo, block, hi], axis=dy)
    size_x = block.shape[dx]
    (lo,), (hi,) = swap(
        "gx",
        [lax.slice_in_dim(block, size_x - hx, size_x, axis=dx)],
        [lax.slice_in_dim(block, 0, hx, axis=dx)],
    )
    return jnp.concatenate([lo, block, hi], axis=dx)


def zpad(a):
    return jnp.pad(a, [(0, 0)] * (a.ndim - 1) + [(1, 1)])


def near_sum(wide):
    padded = zpad(wide)
    total = wide[..., 2:, 1:-1, :] + wide[..., :-2, 1:-1, :]
    total = total + wide[..., 1:-1, 2:, :] + wide[..., 1:-1, :-2, :]
    total = total + padded[..., 1:-1, 1:-1, 2:] + padded[..., 1:-1, 1:-1, :-2]
    return total


def lookup(grain_ids, table):
    result = jnp.zeros(grain_ids.shape, jnp.float32)
    for index in range(NMAT):
        result = result + (grain_ids == index).astype(jnp.float32) * table[index]
    return result


def body(magnet, grain_ids, exch_table, sat_table, surface_map, near_list, near_blocks):
    cells_x = magnet.shape[1]
    cells_y = magnet.shape[2]
    cells_z = magnet.shape[3]
    grid_x = cells_x * lax.axis_size("gx")
    grid_y = cells_y * lax.axis_size("gy")
    base_x = lax.axis_index("gx") * cells_x
    base_y = lax.axis_index("gy") * cells_y

    def inside(h):
        xs = base_x - h + jnp.arange(cells_x + 2 * h, dtype=jnp.int32)
        ys = base_y - h + jnp.arange(cells_y + 2 * h, dtype=jnp.int32)
        ok_x = (xs >= 0) & (xs < grid_x)
        ok_y = (ys >= 0) & (ys < grid_y)
        return (ok_x[:, None] & ok_y[None, :])[:, :, None]

    halo = SWEEPS
    data = jnp.concatenate([magnet, grain_ids.astype(jnp.float32)[None]], axis=0)
    wide = widen(data, halo, halo, 1, 2)
    m0, m1, m2 = wide[0], wide[1], wide[2]
    exch_coef = lookup(grain_ids, exch_table)

    hs = halo - 1
    ex = slice(1, 1 + cells_x + 2 * hs)
    ey = slice(1, 1 + cells_y + 2 * hs)
    m2p = zpad(m2[ex, ey])
    diverge = (
        m0[2 : 2 + cells_x + 2 * hs, ey]
        - m0[0 : cells_x + 2 * hs, ey]
        + m1[ex, 2 : 2 + cells_y + 2 * hs]
        - m1[ex, 0 : cells_y + 2 * hs]
        + m2p[:, :, 2:]
        - m2p[:, :, :-2]
    ) * 0.5
    sat_w = lookup(wide[3, ex, ey].astype(jnp.int32), sat_table)
    source = -sat_w * diverge

    scalar = jnp.where(inside(hs), source / DIAG, 0.0)
    for sweep in range(1, SWEEPS):
        h = hs - sweep
        off = hs - h
        src = source[off : off + cells_x + 2 * h, off : off + cells_y + 2 * h]
        value = (near_sum(scalar) + src) / DIAG
        scalar = jnp.where(inside(h), value, 0.0) if h > 0 else value

    mag_1 = wide[0:3, halo - 1 : halo + 1 + cells_x, halo - 1 : halo + 1 + cells_y]
    laplace = near_sum(mag_1) - 6.0 * magnet

    node_map = surface_map[:, 0, :]
    cell_ids = jnp.arange(cells_x * cells_y, dtype=jnp.int32)
    onehot = node_map[:, :, None] == cell_ids[None, None, :]
    face_vals = jnp.stack([scalar[:, :, 0], scalar[:, :, -1]]).reshape(2, cells_x * cells_y)
    panels = jnp.sum(jnp.where(onehot, face_vals[:, None, :], 0.0), axis=2)
    low_panels = panels.astype(jnp.bfloat16)
    local_list = near_list[0]
    blank_pick = jnp.zeros((local_list.shape[0], local_list.shape[1], NODES), jnp.bfloat16)
    group = lax.axis_size("gy")
    copies = jnp.broadcast_to(low_panels[None], (group,) + low_panels.shape)
    piece = lax.all_to_all(copies, "gy", 0, 0, tiled=True).reshape(group * 2, NODES)
    valid = (local_list >= 0) & (local_list < piece.shape[0])
    picked = piece[jnp.clip(local_list, 0, piece.shape[0] - 1)]
    chosen = jnp.where(valid[:, :, None], picked, blank_pick)
    double = (
        jnp.einsum("tkij,tkj->ti", near_blocks[0], chosen, preferred_element_type=jnp.float32)
        - 0.5 * panels
    )
    cells = jnp.sum(jnp.where(onehot, double[:, :, None], 0.0), axis=1)
    planes = cells.reshape(2, cells_x, cells_y)

    he = EXT_SWEEPS + 1
    (p_lo, s_lo), (p_hi, s_hi) = swap(
        "gx",
        [planes[:, cells_x - he :], scalar[cells_x - 1 :]],
        [planes[:, :he], scalar[:1]],
    )
    planes_x = jnp.concatenate([p_lo, planes, p_hi], axis=1)
    (q_lo, t_lo), (q_hi, t_hi) = swap(
        "gy",
        [planes_x[:, :, cells_y - he :], scalar[:, cells_y - 1 :]],
        [planes_x[:, :, :he], scalar[:, :1]],
    )
    planes_w = jnp.concatenate([q_lo, planes_x, q_hi], axis=2)

    column = jnp.concatenate([s_lo, scalar, s_hi], axis=0)
    row_pad = ((1, 1), (0, 0), (0, 0))
    scalar_1 = jnp.concatenate([jnp.pad(t_lo, row_pad), column, jnp.pad(t_hi, row_pad)], axis=1)

    z_ids = jnp.arange(cells_z, dtype=jnp.int32)
    bottom = z_ids == 0
    top = z_ids == cells_z - 1
    zero_w = jnp.zeros_like(planes_w[0])

    def reset(values, off, size_x, size_y):
        sub = planes_w[:, off : off + size_x, off : off + size_y]
        zero = zero_w[off : off + size_x, off : off + size_y]
        lower = jnp.stack([sub[0], zero])[..., None]
        upper = jnp.stack([zero, sub[1]])[..., None]
        return jnp.where(bottom, lower, jnp.where(top, upper, values))

    extend = reset(
        jnp.zeros((2,) + planes_w.shape[1:] + (cells_z,), jnp.float32),
        0,
        planes_w.shape[1],
        planes_w.shape[2],
    )
    for sweep in range(EXT_SWEEPS):
        h = he - 1 - sweep
        off = he - h
        value = jnp.where(inside(h), near_sum(extend) / DIAG, 0.0)
        extend = reset(value, off, cells_x + 2 * h, cells_y + 2 * h)

    potential_1 = scalar_1 + extend[0] + extend[1]
    potential = potential_1[1:-1, 1:-1]
    padded = zpad(potential_1)
    grad_x = (potential_1[2:, 1:-1] - potential_1[:-2, 1:-1]) * 0.5
    grad_y = (potential_1[1:-1, 2:] - potential_1[1:-1, :-2]) * 0.5
    grad_z = (padded[1:-1, 1:-1, 2:] - padded[1:-1, 1:-1, :-2]) * 0.5
    field = exch_coef[None] * laplace - jnp.stack([grad_x, grad_y, grad_z])
    return (field, potential)


def solution(mesh):
    return jax.shard_map(
        body,
        mesh=mesh,
        in_specs=(
            P(None, "gx", "gy", None),
            P("gx", "gy", None),
            P(),
            P(),
            P("gx", "gy", None),
            P("gx", "gy", None),
            P("gx", "gy", None, None, None),
        ),
        out_specs=(P(None, "gx", "gy", None), P("gx", "gy", None)),
        check_vma=False,
    )
```

```python
import jax
import jax.numpy as jnp
from jax import lax
from jax.sharding import PartitionSpec as P

NODES = 128
SWEEPS = 8
EXT_SWEEPS = 4
NMAT = 4


SCREEN = 0.25
DIAG = 6.0 + SCREEN


def _pairs(count, step):
    return [(i, i + step) for i in range(count) if 0 <= i + step < count]


def _pack(arrays):
    return jnp.concatenate([a.reshape(-1) for a in arrays])


def _unpack(flat, like):
    out = []
    start = 0
    for a in like:
        out.append(flat[start : start + a.size].reshape(a.shape))
        start += a.size
    return out


def swap(axis, to_next, to_prev):
    count = lax.axis_size(axis)
    if len(to_next) == 1:
        from_prev = [lax.ppermute(to_next[0], axis, _pairs(count, 1))]
        from_next = [lax.ppermute(to_prev[0], axis, _pairs(count, -1))]
        return from_prev, from_next
    from_prev = lax.ppermute(_pack(to_next), axis, _pairs(count, 1))
    from_next = lax.ppermute(_pack(to_prev), axis, _pairs(count, -1))
    return _unpack(from_prev, to_next), _unpack(from_next, to_prev)


def widen(block, hx, hy, dx, dy, trim=0):
    size_x = block.shape[dx]
    (lo,), (hi,) = swap(
        "gx",
        [lax.slice_in_dim(block, size_x - hx, size_x, axis=dx)],
        [lax.slice_in_dim(block, 0, hx, axis=dx)],
    )
    block = jnp.concatenate([lo, block, hi], axis=dx)
    size_y = block.shape[dy]
    width = block.shape[dx]
    inner = lax.slice_in_dim(block, trim, width - trim, axis=dx)
    (lo,), (hi,) = swap(
        "gy",
        [lax.slice_in_dim(inner, size_y - hy, size_y, axis=dy)],
        [lax.slice_in_dim(inner, 0, hy, axis=dy)],
    )
    pad = [(0, 0)] * block.ndim
    pad[dx] = (trim, trim)
    return jnp.concatenate([jnp.pad(lo, pad), block, jnp.pad(hi, pad)], axis=dy)


def zpad(a):
    return jnp.pad(a, [(0, 0)] * (a.ndim - 1) + [(1, 1)])


def near_sum(wide):
    padded = zpad(wide)
    total = wide[..., 2:, 1:-1, :] + wide[..., :-2, 1:-1, :]
    total = total + wide[..., 1:-1, 2:, :] + wide[..., 1:-1, :-2, :]
    total = total + padded[..., 1:-1, 1:-1, 2:] + padded[..., 1:-1, 1:-1, :-2]
    return total


def lookup(grain_ids, table):
    result = jnp.zeros(grain_ids.shape, jnp.float32)
    for index in range(NMAT):
        result = result + (grain_ids == index).astype(jnp.float32) * table[index]
    return result


def body(magnet, grain_ids, exch_table, sat_table, surface_map, near_list, near_blocks):
    cells_x = magnet.shape[1]
    cells_y = magnet.shape[2]
    cells_z = magnet.shape[3]
    grid_x = cells_x * lax.axis_size("gx")
    grid_y = cells_y * lax.axis_size("gy")
    base_x = lax.axis_index("gx") * cells_x
    base_y = lax.axis_index("gy") * cells_y

    def inside(h):
        xs = base_x - h + jnp.arange(cells_x + 2 * h, dtype=jnp.int32)
        ys = base_y - h + jnp.arange(cells_y + 2 * h, dtype=jnp.int32)
        ok_x = (xs >= 0) & (xs < grid_x)
        ok_y = (ys >= 0) & (ys < grid_y)
        return (ok_x[:, None] & ok_y[None, :])[:, :, None]

    halo = SWEEPS
    data = jnp.concatenate([magnet, grain_ids.astype(jnp.float32)[None]], axis=0)
    wide = widen(data, halo, halo, 1, 2, trim=1)
    m0, m1, m2 = wide[0], wide[1], wide[2]
    exch_coef = lookup(grain_ids, exch_table)

    hs = halo - 1
    ex = slice(1, 1 + cells_x + 2 * hs)
    ey = slice(1, 1 + cells_y + 2 * hs)
    m2p = zpad(m2[ex, ey])
    diverge = (
        m0[2 : 2 + cells_x + 2 * hs, ey]
        - m0[0 : cells_x + 2 * hs, ey]
        + m1[ex, 2 : 2 + cells_y + 2 * hs]
        - m1[ex, 0 : cells_y + 2 * hs]
        + m2p[:, :, 2:]
        - m2p[:, :, :-2]
    ) * 0.5
    sat_w = lookup(wide[3, ex, ey].astype(jnp.int32), sat_table)
    source = -sat_w * diverge

    scalar = jnp.where(inside(hs), source / DIAG, 0.0)
    for sweep in range(1, SWEEPS):
        h = hs - sweep
        off = hs - h
        src = source[off : off + cells_x + 2 * h, off : off + cells_y + 2 * h]
        value = (near_sum(scalar) + src) / DIAG
        scalar = jnp.where(inside(h), value, 0.0) if h > 0 else value

    mag_1 = wide[0:3, halo - 1 : halo + 1 + cells_x, halo - 1 : halo + 1 + cells_y]
    laplace = near_sum(mag_1) - 6.0 * magnet

    node_map = surface_map[:, 0, :]
    cell_ids = jnp.arange(cells_x * cells_y, dtype=jnp.int32)
    onehot = node_map[:, :, None] == cell_ids[None, None, :]
    face_vals = jnp.stack([scalar[:, :, 0], scalar[:, :, -1]]).reshape(2, cells_x * cells_y)
    panels = jnp.sum(jnp.where(onehot, face_vals[:, None, :], 0.0), axis=2)
    low_panels = panels.astype(jnp.bfloat16)
    local_list = near_list[0]
    blank_pick = jnp.zeros((local_list.shape[0], local_list.shape[1], NODES), jnp.bfloat16)
    group = lax.axis_size("gy")
    copies = jnp.broadcast_to(low_panels[None], (group,) + low_panels.shape)
    piece = lax.all_to_all(copies, "gy", 0, 0, tiled=True).reshape(group * 2, NODES)
    valid = (local_list >= 0) & (local_list < piece.shape[0])
    picked = piece[jnp.clip(local_list, 0, piece.shape[0] - 1)]
    chosen = jnp.where(valid[:, :, None], picked, blank_pick)
    double = (
        jnp.einsum("tkij,tkj->ti", near_blocks[0], chosen, preferred_element_type=jnp.float32)
        - 0.5 * panels
    )
    cells = jnp.sum(jnp.where(onehot, double[:, :, None], 0.0), axis=1)
    planes = cells.reshape(2, cells_x, cells_y)

    he = EXT_SWEEPS + 1
    (q_lo, t_lo), (q_hi, t_hi) = swap(
        "gy",
        [planes[:, :, cells_y - he :], scalar[:, cells_y - 1 :]],
        [planes[:, :, :he], scalar[:, :1]],
    )
    planes_y = jnp.concatenate([q_lo, planes, q_hi], axis=2)
    (p_lo, s_lo), (p_hi, s_hi) = swap(
        "gx",
        [planes_y[:, cells_x - he :], scalar[cells_x - 1 :]],
        [planes_y[:, :he], scalar[:1]],
    )
    planes_w = jnp.concatenate([p_lo, planes_y, p_hi], axis=1)

    column = jnp.concatenate([s_lo, scalar, s_hi], axis=0)
    row_pad = ((1, 1), (0, 0), (0, 0))
    scalar_1 = jnp.concatenate([jnp.pad(t_lo, row_pad), column, jnp.pad(t_hi, row_pad)], axis=1)

    z_ids = jnp.arange(cells_z, dtype=jnp.int32)
    bottom = z_ids == 0
    top = z_ids == cells_z - 1
    zero_w = jnp.zeros_like(planes_w[0])

    def reset(values, off, size_x, size_y):
        sub = planes_w[:, off : off + size_x, off : off + size_y]
        zero = zero_w[off : off + size_x, off : off + size_y]
        lower = jnp.stack([sub[0], zero])[..., None]
        upper = jnp.stack([zero, sub[1]])[..., None]
        return jnp.where(bottom, lower, jnp.where(top, upper, values))

    extend = reset(
        jnp.zeros((2,) + planes_w.shape[1:] + (cells_z,), jnp.float32),
        0,
        planes_w.shape[1],
        planes_w.shape[2],
    )
    for sweep in range(EXT_SWEEPS):
        h = he - 1 - sweep
        off = he - h
        value = jnp.where(inside(h), near_sum(extend) / DIAG, 0.0)
        extend = reset(value, off, cells_x + 2 * h, cells_y + 2 * h)

    potential_1 = scalar_1 + extend[0] + extend[1]
    potential = potential_1[1:-1, 1:-1]
    padded = zpad(potential_1)
    grad_x = (potential_1[2:, 1:-1] - potential_1[:-2, 1:-1]) * 0.5
    grad_y = (potential_1[1:-1, 2:] - potential_1[1:-1, :-2]) * 0.5
    grad_z = (padded[1:-1, 1:-1, 2:] - padded[1:-1, 1:-1, :-2]) * 0.5
    field = exch_coef[None] * laplace - jnp.stack([grad_x, grad_y, grad_z])
    return (field, potential)


def solution(mesh):
    return jax.shard_map(
        body,
        mesh=mesh,
        in_specs=(
            P(None, "gx", "gy", None),
            P("gx", "gy", None),
            P(),
            P(),
            P("gx", "gy", None),
            P("gx", "gy", None),
            P("gx", "gy", None, None, None),
        ),
        out_specs=(P(None, "gx", "gy", None), P("gx", "gy", None)),
        check_vma=False,
    )
```

```python
import jax
import jax.numpy as jnp
from jax import lax
from jax.sharding import PartitionSpec as P

NODES = 128
SWEEPS = 8
EXT_SWEEPS = 4
NMAT = 4


SCREEN = 0.25
DIAG = 6.0 + SCREEN


def _pairs(count, step):
    return [(i, i + step) for i in range(count) if 0 <= i + step < count]


def _pack(arrays):
    return jnp.concatenate([a.reshape(-1) for a in arrays])


def _unpack(flat, like):
    out = []
    start = 0
    for a in like:
        out.append(flat[start : start + a.size].reshape(a.shape))
        start += a.size
    return out


def swap(axis, to_next, to_prev):
    count = lax.axis_size(axis)
    if len(to_next) == 1:
        from_prev = [lax.ppermute(to_next[0], axis, _pairs(count, 1))]
        from_next = [lax.ppermute(to_prev[0], axis, _pairs(count, -1))]
        return from_prev, from_next
    from_prev = lax.ppermute(_pack(to_next), axis, _pairs(count, 1))
    from_next = lax.ppermute(_pack(to_prev), axis, _pairs(count, -1))
    return _unpack(from_prev, to_next), _unpack(from_next, to_prev)


def widen(block, hx, hy, dx, dy):
    size_x = block.shape[dx]
    (lo,), (hi,) = swap(
        "gx",
        [lax.slice_in_dim(block, size_x - hx, size_x, axis=dx)],
        [lax.slice_in_dim(block, 0, hx, axis=dx)],
    )
    block = jnp.concatenate([lo, block, hi], axis=dx)
    size_y = block.shape[dy]
    (lo,), (hi,) = swap(
        "gy",
        [lax.slice_in_dim(block, size_y - hy, size_y, axis=dy)],
        [lax.slice_in_dim(block, 0, hy, axis=dy)],
    )
    return jnp.concatenate([lo, block, hi], axis=dy)


def zpad(a):
    return jnp.pad(a, [(0, 0)] * (a.ndim - 1) + [(1, 1)])


def near_sum(wide):
    padded = zpad(wide)
    total = wide[..., 2:, 1:-1, :] + wide[..., :-2, 1:-1, :]
    total = total + wide[..., 1:-1, 2:, :] + wide[..., 1:-1, :-2, :]
    total = total + padded[..., 1:-1, 1:-1, 2:] + padded[..., 1:-1, 1:-1, :-2]
    return total


def lookup(grain_ids, table):
    result = jnp.zeros(grain_ids.shape, jnp.float32)
    for index in range(NMAT):
        result = result + (grain_ids == index).astype(jnp.float32) * table[index]
    return result


def body(magnet, grain_ids, exch_table, sat_table, surface_map, near_list, near_blocks):
    cells_x = magnet.shape[1]
    cells_y = magnet.shape[2]
    cells_z = magnet.shape[3]
    grid_x = cells_x * lax.axis_size("gx")
    grid_y = cells_y * lax.axis_size("gy")
    base_x = lax.axis_index("gx") * cells_x
    base_y = lax.axis_index("gy") * cells_y

    def inside(h):
        xs = base_x - h + jnp.arange(cells_x + 2 * h, dtype=jnp.int32)
        ys = base_y - h + jnp.arange(cells_y + 2 * h, dtype=jnp.int32)
        ok_x = (xs >= 0) & (xs < grid_x)
        ok_y = (ys >= 0) & (ys < grid_y)
        return (ok_x[:, None] & ok_y[None, :])[:, :, None]

    halo = SWEEPS
    data = jnp.concatenate([magnet, grain_ids.astype(jnp.float32)[None]], axis=0)
    wide = widen(data, halo, halo, 1, 2)
    m0, m1, m2 = wide[0], wide[1], wide[2]
    exch_coef = lookup(grain_ids, exch_table)

    hs = halo - 1
    ex = slice(1, 1 + cells_x + 2 * hs)
    ey = slice(1, 1 + cells_y + 2 * hs)
    m2p = zpad(m2[ex, ey])
    diverge = (
        m0[2 : 2 + cells_x + 2 * hs, ey]
        - m0[0 : cells_x + 2 * hs, ey]
        + m1[ex, 2 : 2 + cells_y + 2 * hs]
        - m1[ex, 0 : cells_y + 2 * hs]
        + m2p[:, :, 2:]
        - m2p[:, :, :-2]
    ) * 0.5
    sat_w = lookup(wide[3, ex, ey].astype(jnp.int32), sat_table)
    source = -sat_w * diverge

    scalar = jnp.where(inside(hs), source / DIAG, 0.0)
    for sweep in range(1, SWEEPS):
        h = hs - sweep
        off = hs - h
        src = source[off : off + cells_x + 2 * h, off : off + cells_y + 2 * h]
        value = (near_sum(scalar) + src) / DIAG
        scalar = jnp.where(inside(h), value, 0.0) if h > 0 else value

    mag_1 = wide[0:3, halo - 1 : halo + 1 + cells_x, halo - 1 : halo + 1 + cells_y]
    laplace = near_sum(mag_1) - 6.0 * magnet

    node_map = surface_map[:, 0, :]
    cell_ids = jnp.arange(cells_x * cells_y, dtype=jnp.int32)
    onehot = node_map[:, :, None] == cell_ids[None, None, :]
    face_vals = jnp.stack([scalar[:, :, 0], scalar[:, :, -1]]).reshape(2, cells_x * cells_y)
    panels = jnp.sum(jnp.where(onehot, face_vals[:, None, :], 0.0), axis=2)
    low_panels = panels.astype(jnp.bfloat16)
    local_list = near_list[0]
    blank_pick = jnp.zeros((local_list.shape[0], local_list.shape[1], NODES), jnp.bfloat16)
    group = lax.axis_size("gy")
    copies = jnp.broadcast_to(low_panels[None], (group,) + low_panels.shape)
    piece = lax.all_to_all(copies, "gy", 0, 0, tiled=True).reshape(group * 2, NODES)
    valid = (local_list >= 0) & (local_list < piece.shape[0])
    picked = piece[jnp.clip(local_list, 0, piece.shape[0] - 1)]
    chosen = jnp.where(valid[:, :, None], picked, blank_pick)
    double = (
        jnp.einsum("tkij,tkj->ti", near_blocks[0], chosen, preferred_element_type=jnp.float32)
        - 0.5 * panels
    )
    cells = jnp.sum(jnp.where(onehot, double[:, :, None], 0.0), axis=1)
    planes = cells.reshape(2, cells_x, cells_y)

    he = EXT_SWEEPS + 1
    (q_lo, t_lo), (q_hi, t_hi) = swap(
        "gy",
        [planes[:, :, cells_y - he :], scalar[:, cells_y - 1 :]],
        [planes[:, :, :he], scalar[:, :1]],
    )
    planes_y = jnp.concatenate([q_lo, planes, q_hi], axis=2)
    (p_lo, s_lo), (p_hi, s_hi) = swap(
        "gx",
        [planes_y[:, cells_x - he :], scalar[cells_x - 1 :]],
        [planes_y[:, :he], scalar[:1]],
    )
    planes_w = jnp.concatenate([p_lo, planes_y, p_hi], axis=1)

    column = jnp.concatenate([s_lo, scalar, s_hi], axis=0)
    row_pad = ((1, 1), (0, 0), (0, 0))
    scalar_1 = jnp.concatenate([jnp.pad(t_lo, row_pad), column, jnp.pad(t_hi, row_pad)], axis=1)

    z_ids = jnp.arange(cells_z, dtype=jnp.int32)
    bottom = z_ids == 0
    top = z_ids == cells_z - 1
    zero_w = jnp.zeros_like(planes_w[0])

    def reset(values, off, size_x, size_y):
        sub = planes_w[:, off : off + size_x, off : off + size_y]
        zero = zero_w[off : off + size_x, off : off + size_y]
        lower = jnp.stack([sub[0], zero])[..., None]
        upper = jnp.stack([zero, sub[1]])[..., None]
        return jnp.where(bottom, lower, jnp.where(top, upper, values))

    extend = reset(
        jnp.zeros((2,) + planes_w.shape[1:] + (cells_z,), jnp.float32),
        0,
        planes_w.shape[1],
        planes_w.shape[2],
    )
    for sweep in range(EXT_SWEEPS):
        h = he - 1 - sweep
        off = he - h
        value = jnp.where(inside(h), near_sum(extend) / DIAG, 0.0)
        extend = reset(value, off, cells_x + 2 * h, cells_y + 2 * h)

    potential_1 = scalar_1 + extend[0] + extend[1]
    potential = potential_1[1:-1, 1:-1]
    padded = zpad(potential_1)
    grad_x = (potential_1[2:, 1:-1] - potential_1[:-2, 1:-1]) * 0.5
    grad_y = (potential_1[1:-1, 2:] - potential_1[1:-1, :-2]) * 0.5
    grad_z = (padded[1:-1, 1:-1, 2:] - padded[1:-1, 1:-1, :-2]) * 0.5
    field = exch_coef[None] * laplace - jnp.stack([grad_x, grad_y, grad_z])
    return (field, potential)


def solution(mesh):
    return jax.shard_map(
        body,
        mesh=mesh,
        in_specs=(
            P(None, "gx", "gy", None),
            P("gx", "gy", None),
            P(),
            P(),
            P("gx", "gy", None),
            P("gx", "gy", None),
            P("gx", "gy", None, None, None),
        ),
        out_specs=(P(None, "gx", "gy", None), P("gx", "gy", None)),
        check_vma=False,
    )
```

```python
import jax
import jax.numpy as jnp
from jax import lax
from jax.sharding import PartitionSpec as P

NODES = 128
SWEEPS = 8
EXT_SWEEPS = 4
NMAT = 4


SCREEN = 0.25
DIAG = 6.0 + SCREEN


def _pairs(count, step):
    return [(i, i + step) for i in range(count) if 0 <= i + step < count]


def _pack(arrays):
    return jnp.concatenate([a.reshape(-1) for a in arrays])


def _unpack(flat, like):
    out = []
    start = 0
    for a in like:
        out.append(flat[start : start + a.size].reshape(a.shape))
        start += a.size
    return out


def swap(axis, to_next, to_prev):
    count = lax.axis_size(axis)
    if len(to_next) == 1:
        from_prev = [lax.ppermute(to_next[0], axis, _pairs(count, 1))]
        from_next = [lax.ppermute(to_prev[0], axis, _pairs(count, -1))]
        return from_prev, from_next
    from_prev = lax.ppermute(_pack(to_next), axis, _pairs(count, 1))
    from_next = lax.ppermute(_pack(to_prev), axis, _pairs(count, -1))
    return _unpack(from_prev, to_next), _unpack(from_next, to_prev)


def widen(block, hx, hy, dx, dy):
    size_x = block.shape[dx]
    (lo,), (hi,) = swap(
        "gx",
        [lax.slice_in_dim(block, size_x - hx, size_x, axis=dx)],
        [lax.slice_in_dim(block, 0, hx, axis=dx)],
    )
    block = jnp.concatenate([lo, block, hi], axis=dx)
    size_y = block.shape[dy]
    (lo,), (hi,) = swap(
        "gy",
        [lax.slice_in_dim(block, size_y - hy, size_y, axis=dy)],
        [lax.slice_in_dim(block, 0, hy, axis=dy)],
    )
    return jnp.concatenate([lo, block, hi], axis=dy)


def zpad(a):
    return jnp.pad(a, [(0, 0)] * (a.ndim - 1) + [(1, 1)])


def near_sum(wide):
    padded = zpad(wide)
    total = wide[..., 2:, 1:-1, :] + wide[..., :-2, 1:-1, :]
    total = total + wide[..., 1:-1, 2:, :] + wide[..., 1:-1, :-2, :]
    total = total + padded[..., 1:-1, 1:-1, 2:] + padded[..., 1:-1, 1:-1, :-2]
    return total


def lookup(grain_ids, table):
    result = jnp.zeros(grain_ids.shape, jnp.float32)
    for index in range(NMAT):
        result = result + (grain_ids == index).astype(jnp.float32) * table[index]
    return result


def body(magnet, grain_ids, exch_table, sat_table, surface_map, near_list, near_blocks):
    cells_x = magnet.shape[1]
    cells_y = magnet.shape[2]
    cells_z = magnet.shape[3]
    grid_x = cells_x * lax.axis_size("gx")
    grid_y = cells_y * lax.axis_size("gy")
    base_x = lax.axis_index("gx") * cells_x
    base_y = lax.axis_index("gy") * cells_y

    def inside(h):
        xs = base_x - h + jnp.arange(cells_x + 2 * h, dtype=jnp.int32)
        ys = base_y - h + jnp.arange(cells_y + 2 * h, dtype=jnp.int32)
        ok_x = (xs >= 0) & (xs < grid_x)
        ok_y = (ys >= 0) & (ys < grid_y)
        return (ok_x[:, None] & ok_y[None, :])[:, :, None]

    he = EXT_SWEEPS + 1
    node_map = surface_map[:, 0, :]
    cell_ids = jnp.arange(cells_x * cells_y, dtype=jnp.int32)
    onehot = node_map[:, :, None] == cell_ids[None, None, :]
    y_major = (cell_ids % cells_x) * cells_y + cell_ids // cells_x
    onehot_y = node_map[:, :, None] == y_major[None, None, :]
    rows = jnp.einsum(
        "tnc,tknj->tkcj",
        onehot_y.astype(near_blocks.dtype),
        near_blocks[0],
        preferred_element_type=jnp.float32,
    ).astype(near_blocks.dtype)
    rows = rows.reshape(rows.shape[0], rows.shape[1], cells_y, cells_x, NODES)
    (rows_lo,), (rows_hi,) = swap("gy", [rows[:, :, cells_y - he :]], [rows[:, :, :he]])

    halo = SWEEPS
    data = jnp.concatenate([magnet, grain_ids.astype(jnp.float32)[None]], axis=0)
    wide = widen(data, halo, halo, 1, 2)
    m0, m1, m2 = wide[0], wide[1], wide[2]
    exch_coef = lookup(grain_ids, exch_table)

    hs = halo - 1
    ex = slice(1, 1 + cells_x + 2 * hs)
    ey = slice(1, 1 + cells_y + 2 * hs)
    m2p = zpad(m2[ex, ey])
    diverge = (
        m0[2 : 2 + cells_x + 2 * hs, ey]
        - m0[0 : cells_x + 2 * hs, ey]
        + m1[ex, 2 : 2 + cells_y + 2 * hs]
        - m1[ex, 0 : cells_y + 2 * hs]
        + m2p[:, :, 2:]
        - m2p[:, :, :-2]
    ) * 0.5
    sat_w = lookup(wide[3, ex, ey].astype(jnp.int32), sat_table)
    source = -sat_w * diverge

    scalar = jnp.where(inside(hs), source / DIAG, 0.0)
    for sweep in range(1, SWEEPS):
        h = hs - sweep
        off = hs - h
        src = source[off : off + cells_x + 2 * h, off : off + cells_y + 2 * h]
        value = (near_sum(scalar) + src) / DIAG
        scalar = jnp.where(inside(h), value, 0.0) if h > 0 else value

    mag_1 = wide[0:3, halo - 1 : halo + 1 + cells_x, halo - 1 : halo + 1 + cells_y]
    laplace = near_sum(mag_1) - 6.0 * magnet

    face = jnp.stack([scalar[:, :, 0], scalar[:, :, -1]])
    face_flat = face.reshape(2, cells_x * cells_y)
    panels = jnp.sum(jnp.where(onehot, face_flat[:, None, :], 0.0), axis=2)
    local_list = near_list[0]

    group = lax.axis_size("gy")
    me = lax.axis_index("gy")
    list_f = local_list.astype(jnp.float32)
    side_hi = _pack([list_f, face[:, :, cells_y - he :], scalar[:, cells_y - 1]])
    side_lo = _pack([list_f, face[:, :, :he], scalar[:, 0]])
    rel = jnp.arange(group, dtype=jnp.int32)[:, None] - me
    side = jnp.where(rel == 1, side_hi[None], jnp.where(rel == -1, side_lo[None], 0.0))
    chunks = jnp.concatenate(
        [jnp.broadcast_to(panels.reshape(1, -1), (group, panels.size)), side], axis=1
    )
    got = lax.all_to_all(chunks, "gy", 0, 0, tiled=True)
    piece = got[:, : panels.size].reshape(group * 2, NODES).astype(jnp.bfloat16)
    from_lo = jnp.where(me > 0, got[jnp.maximum(me - 1, 0), panels.size :], 0.0)
    from_hi = jnp.where(me < group - 1, got[jnp.minimum(me + 1, group - 1), panels.size :], 0.0)
    like = [list_f, face[:, :, :he], scalar[:, 0]]
    list_lo, face_lo, t_lo = _unpack(from_lo, like)
    list_hi, face_hi, t_hi = _unpack(from_hi, like)

    def double_of(block_rows, lists, faces):
        lists = lists.astype(jnp.int32)
        valid = (lists >= 0) & (lists < piece.shape[0])
        picked = piece[jnp.clip(lists, 0, piece.shape[0] - 1)]
        chosen = jnp.where(valid[:, :, None], picked, jnp.zeros_like(picked))
        product = jnp.einsum(
            "tkyxj,tkj->txy", block_rows, chosen, preferred_element_type=jnp.float32
        )
        return product - 0.5 * faces

    planes_y = jnp.concatenate(
        [
            double_of(rows_lo, list_lo, face_lo),
            double_of(rows, local_list, face),
            double_of(rows_hi, list_hi, face_hi),
        ],
        axis=2,
    )

    (p_lo, s_lo), (p_hi, s_hi) = swap(
        "gx",
        [planes_y[:, cells_x - he :], scalar[cells_x - 1 :]],
        [planes_y[:, :he], scalar[:1]],
    )
    planes_w = jnp.concatenate([p_lo, planes_y, p_hi], axis=1)
    t_lo = t_lo[:, None]
    t_hi = t_hi[:, None]

    column = jnp.concatenate([s_lo, scalar, s_hi], axis=0)
    row_pad = ((1, 1), (0, 0), (0, 0))
    scalar_1 = jnp.concatenate([jnp.pad(t_lo, row_pad), column, jnp.pad(t_hi, row_pad)], axis=1)

    z_ids = jnp.arange(cells_z, dtype=jnp.int32)
    bottom = z_ids == 0
    top = z_ids == cells_z - 1
    zero_w = jnp.zeros_like(planes_w[0])

    def reset(values, off, size_x, size_y):
        sub = planes_w[:, off : off + size_x, off : off + size_y]
        zero = zero_w[off : off + size_x, off : off + size_y]
        lower = jnp.stack([sub[0], zero])[..., None]
        upper = jnp.stack([zero, sub[1]])[..., None]
        return jnp.where(bottom, lower, jnp.where(top, upper, values))

    extend = reset(
        jnp.zeros((2,) + planes_w.shape[1:] + (cells_z,), jnp.float32),
        0,
        planes_w.shape[1],
        planes_w.shape[2],
    )
    for sweep in range(EXT_SWEEPS):
        h = he - 1 - sweep
        off = he - h
        value = jnp.where(inside(h), near_sum(extend) / DIAG, 0.0)
        extend = reset(value, off, cells_x + 2 * h, cells_y + 2 * h)

    potential_1 = scalar_1 + extend[0] + extend[1]
    potential = potential_1[1:-1, 1:-1]
    padded = zpad(potential_1)
    grad_x = (potential_1[2:, 1:-1] - potential_1[:-2, 1:-1]) * 0.5
    grad_y = (potential_1[1:-1, 2:] - potential_1[1:-1, :-2]) * 0.5
    grad_z = (padded[1:-1, 1:-1, 2:] - padded[1:-1, 1:-1, :-2]) * 0.5
    field = exch_coef[None] * laplace - jnp.stack([grad_x, grad_y, grad_z])
    return (field, potential)


def solution(mesh):
    return jax.shard_map(
        body,
        mesh=mesh,
        in_specs=(
            P(None, "gx", "gy", None),
            P("gx", "gy", None),
            P(),
            P(),
            P("gx", "gy", None),
            P("gx", "gy", None),
            P("gx", "gy", None, None, None),
        ),
        out_specs=(P(None, "gx", "gy", None), P("gx", "gy", None)),
        check_vma=False,
    )
```

```python
import jax
import jax.numpy as jnp
from jax import lax
from jax.sharding import PartitionSpec as P

NODES = 128
SWEEPS = 8
EXT_SWEEPS = 4
NMAT = 4


SCREEN = 0.25
DIAG = 6.0 + SCREEN


def _pairs(count, step):
    return [(i, i + step) for i in range(count) if 0 <= i + step < count]


def _pack(arrays):
    return jnp.concatenate([a.reshape(-1) for a in arrays])


def _unpack(flat, like):
    out = []
    start = 0
    for a in like:
        out.append(flat[start : start + a.size].reshape(a.shape))
        start += a.size
    return out


def swap(axis, to_next, to_prev):
    count = lax.axis_size(axis)
    if len(to_next) == 1:
        from_prev = [lax.ppermute(to_next[0], axis, _pairs(count, 1))]
        from_next = [lax.ppermute(to_prev[0], axis, _pairs(count, -1))]
        return from_prev, from_next
    from_prev = lax.ppermute(_pack(to_next), axis, _pairs(count, 1))
    from_next = lax.ppermute(_pack(to_prev), axis, _pairs(count, -1))
    return _unpack(from_prev, to_next), _unpack(from_next, to_prev)


def widen(block, hx, hy, dx, dy):
    size_x = block.shape[dx]
    (lo,), (hi,) = swap(
        "gx",
        [lax.slice_in_dim(block, size_x - hx, size_x, axis=dx)],
        [lax.slice_in_dim(block, 0, hx, axis=dx)],
    )
    block = jnp.concatenate([lo, block, hi], axis=dx)
    size_y = block.shape[dy]
    (lo,), (hi,) = swap(
        "gy",
        [lax.slice_in_dim(block, size_y - hy, size_y, axis=dy)],
        [lax.slice_in_dim(block, 0, hy, axis=dy)],
    )
    return jnp.concatenate([lo, block, hi], axis=dy)


def zpad(a):
    return jnp.pad(a, [(0, 0)] * (a.ndim - 1) + [(1, 1)])


def near_sum(wide):
    padded = zpad(wide)
    total = wide[..., 2:, 1:-1, :] + wide[..., :-2, 1:-1, :]
    total = total + wide[..., 1:-1, 2:, :] + wide[..., 1:-1, :-2, :]
    total = total + padded[..., 1:-1, 1:-1, 2:] + padded[..., 1:-1, 1:-1, :-2]
    return total


def lookup(grain_ids, table):
    result = jnp.full(grain_ids.shape, table[NMAT - 1], jnp.float32)
    for index in range(NMAT - 2, -1, -1):
        result = jnp.where(grain_ids == index, table[index], result)
    return result


def body(magnet, grain_ids, exch_table, sat_table, surface_map, near_list, near_blocks):
    cells_x = magnet.shape[1]
    cells_y = magnet.shape[2]
    cells_z = magnet.shape[3]
    grid_x = cells_x * lax.axis_size("gx")
    grid_y = cells_y * lax.axis_size("gy")
    base_x = lax.axis_index("gx") * cells_x
    base_y = lax.axis_index("gy") * cells_y

    def inside(h):
        xs = base_x - h + jnp.arange(cells_x + 2 * h, dtype=jnp.int32)
        ys = base_y - h + jnp.arange(cells_y + 2 * h, dtype=jnp.int32)
        ok_x = (xs >= 0) & (xs < grid_x)
        ok_y = (ys >= 0) & (ys < grid_y)
        return (ok_x[:, None] & ok_y[None, :])[:, :, None]

    halo = SWEEPS
    data = jnp.concatenate([magnet, grain_ids.astype(jnp.float32)[None]], axis=0)
    wide = widen(data, halo, halo, 1, 2)
    m0, m1, m2 = wide[0], wide[1], wide[2]
    exch_coef = lookup(grain_ids, exch_table)

    hs = halo - 1
    ex = slice(1, 1 + cells_x + 2 * hs)
    ey = slice(1, 1 + cells_y + 2 * hs)
    m2p = zpad(m2[ex, ey])
    diverge = (
        m0[2 : 2 + cells_x + 2 * hs, ey]
        - m0[0 : cells_x + 2 * hs, ey]
        + m1[ex, 2 : 2 + cells_y + 2 * hs]
        - m1[ex, 0 : cells_y + 2 * hs]
        + m2p[:, :, 2:]
        - m2p[:, :, :-2]
    ) * 0.5
    sat_w = lookup(wide[3, ex, ey].astype(jnp.int32), sat_table)
    source = -sat_w * diverge

    scalar = jnp.where(inside(hs), source / DIAG, 0.0)
    for sweep in range(1, SWEEPS):
        h = hs - sweep
        off = hs - h
        src = source[off : off + cells_x + 2 * h, off : off + cells_y + 2 * h]
        value = (near_sum(scalar) + src) / DIAG
        scalar = jnp.where(inside(h), value, 0.0) if h > 0 else value

    mag_1 = wide[0:3, halo - 1 : halo + 1 + cells_x, halo - 1 : halo + 1 + cells_y]
    laplace = near_sum(mag_1) - 6.0 * magnet

    node_map = surface_map[:, 0, :]
    cell_ids = jnp.arange(cells_x * cells_y, dtype=jnp.int32)
    onehot = node_map[:, :, None] == cell_ids[None, None, :]
    face_vals = jnp.stack([scalar[:, :, 0], scalar[:, :, -1]]).reshape(2, cells_x * cells_y)
    panels = jnp.sum(jnp.where(onehot, face_vals[:, None, :], 0.0), axis=2)
    low_panels = panels.astype(jnp.bfloat16)
    local_list = near_list[0]
    blank_pick = jnp.zeros((local_list.shape[0], local_list.shape[1], NODES), jnp.bfloat16)
    group = lax.axis_size("gy")
    copies = jnp.broadcast_to(low_panels[None], (group,) + low_panels.shape)
    piece = lax.all_to_all(copies, "gy", 0, 0, tiled=True).reshape(group * 2, NODES)
    valid = (local_list >= 0) & (local_list < piece.shape[0])
    picked = piece[jnp.clip(local_list, 0, piece.shape[0] - 1)]
    chosen = jnp.where(valid[:, :, None], picked, blank_pick)
    double = (
        jnp.einsum("tkij,tkj->ti", near_blocks[0], chosen, preferred_element_type=jnp.float32)
        - 0.5 * panels
    )
    cells = jnp.sum(jnp.where(onehot, double[:, :, None], 0.0), axis=1)
    planes = cells.reshape(2, cells_x, cells_y)

    he = EXT_SWEEPS + 1
    (p_lo, s_lo), (p_hi, s_hi) = swap(
        "gx",
        [planes[:, cells_x - he :], scalar[cells_x - 1 :]],
        [planes[:, :he], scalar[:1]],
    )
    planes_x = jnp.concatenate([p_lo, planes, p_hi], axis=1)
    (q_lo, t_lo), (q_hi, t_hi) = swap(
        "gy",
        [planes_x[:, :, cells_y - he :], scalar[:, cells_y - 1 :]],
        [planes_x[:, :, :he], scalar[:, :1]],
    )
    planes_w = jnp.concatenate([q_lo, planes_x, q_hi], axis=2)

    column = jnp.concatenate([s_lo, scalar, s_hi], axis=0)
    row_pad = ((1, 1), (0, 0), (0, 0))
    scalar_1 = jnp.concatenate([jnp.pad(t_lo, row_pad), column, jnp.pad(t_hi, row_pad)], axis=1)

    z_ids = jnp.arange(cells_z, dtype=jnp.int32)
    bottom = z_ids == 0
    top = z_ids == cells_z - 1

    def reset(values, off, size_x, size_y):
        sub = planes_w[:, off : off + size_x, off : off + size_y]
        return jnp.where(bottom, sub[0][..., None], jnp.where(top, sub[1][..., None], values))

    extend = reset(
        jnp.zeros(planes_w.shape[1:] + (cells_z,), jnp.float32),
        0,
        planes_w.shape[1],
        planes_w.shape[2],
    )
    for sweep in range(EXT_SWEEPS):
        h = he - 1 - sweep
        off = he - h
        value = jnp.where(inside(h), near_sum(extend) / DIAG, 0.0)
        extend = reset(value, off, cells_x + 2 * h, cells_y + 2 * h)

    potential_1 = scalar_1 + extend
    potential = potential_1[1:-1, 1:-1]
    padded = zpad(potential_1)
    grad_x = (potential_1[2:, 1:-1] - potential_1[:-2, 1:-1]) * 0.5
    grad_y = (potential_1[1:-1, 2:] - potential_1[1:-1, :-2]) * 0.5
    grad_z = (padded[1:-1, 1:-1, 2:] - padded[1:-1, 1:-1, :-2]) * 0.5
    field = exch_coef[None] * laplace - jnp.stack([grad_x, grad_y, grad_z])
    return (field, potential)


def solution(mesh):
    return jax.shard_map(
        body,
        mesh=mesh,
        in_specs=(
            P(None, "gx", "gy", None),
            P("gx", "gy", None),
            P(),
            P(),
            P("gx", "gy", None),
            P("gx", "gy", None),
            P("gx", "gy", None, None, None),
        ),
        out_specs=(P(None, "gx", "gy", None), P("gx", "gy", None)),
        check_vma=False,
    )
```

```python
import jax
import jax.numpy as jnp
from jax import lax
from jax.sharding import PartitionSpec as P

NODES = 128
SWEEPS = 8
EXT_SWEEPS = 4
NMAT = 4


SCREEN = 0.25
DIAG = 6.0 + SCREEN


def _pairs(count, step):
    return [(i, i + step) for i in range(count) if 0 <= i + step < count]


def _pack(arrays):
    return jnp.concatenate([a.reshape(-1) for a in arrays])


def _unpack(flat, like):
    out = []
    start = 0
    for a in like:
        out.append(flat[start : start + a.size].reshape(a.shape))
        start += a.size
    return out


def swap(axis, to_next, to_prev):
    count = lax.axis_size(axis)
    if len(to_next) == 1:
        from_prev = [lax.ppermute(to_next[0], axis, _pairs(count, 1))]
        from_next = [lax.ppermute(to_prev[0], axis, _pairs(count, -1))]
        return from_prev, from_next
    from_prev = lax.ppermute(_pack(to_next), axis, _pairs(count, 1))
    from_next = lax.ppermute(_pack(to_prev), axis, _pairs(count, -1))
    return _unpack(from_prev, to_next), _unpack(from_next, to_prev)


def widen(block, hx, hy, dx, dy):
    size_x = block.shape[dx]
    (lo,), (hi,) = swap(
        "gx",
        [lax.slice_in_dim(block, size_x - hx, size_x, axis=dx)],
        [lax.slice_in_dim(block, 0, hx, axis=dx)],
    )
    block = jnp.concatenate([lo, block, hi], axis=dx)
    size_y = block.shape[dy]
    (lo,), (hi,) = swap(
        "gy",
        [lax.slice_in_dim(block, size_y - hy, size_y, axis=dy)],
        [lax.slice_in_dim(block, 0, hy, axis=dy)],
    )
    return jnp.concatenate([lo, block, hi], axis=dy)


def zpad(a):
    return jnp.pad(a, [(0, 0)] * (a.ndim - 1) + [(1, 1)])


def near_sum(wide):
    padded = zpad(wide)
    total = wide[..., 2:, 1:-1, :] + wide[..., :-2, 1:-1, :]
    total = total + wide[..., 1:-1, 2:, :] + wide[..., 1:-1, :-2, :]
    total = total + padded[..., 1:-1, 1:-1, 2:] + padded[..., 1:-1, 1:-1, :-2]
    return total


def lookup(grain_ids, table):
    result = jnp.full(grain_ids.shape, table[NMAT - 1], jnp.float32)
    for index in range(NMAT - 2, -1, -1):
        result = jnp.where(grain_ids == index, table[index], result)
    return result


def body(magnet, grain_ids, exch_table, sat_table, surface_map, near_list, near_blocks):
    cells_x = magnet.shape[1]
    cells_y = magnet.shape[2]
    cells_z = magnet.shape[3]
    grid_x = cells_x * lax.axis_size("gx")
    grid_y = cells_y * lax.axis_size("gy")
    base_x = lax.axis_index("gx") * cells_x
    base_y = lax.axis_index("gy") * cells_y

    def inside(h):
        xs = base_x - h + jnp.arange(cells_x + 2 * h, dtype=jnp.int32)
        ys = base_y - h + jnp.arange(cells_y + 2 * h, dtype=jnp.int32)
        ok_x = (xs >= 0) & (xs < grid_x)
        ok_y = (ys >= 0) & (ys < grid_y)
        return (ok_x[:, None] & ok_y[None, :])[:, :, None]

    halo = SWEEPS
    channel = lax.broadcasted_iota(jnp.int32, (magnet.shape[0] + 1,) + magnet.shape[1:], 0)
    data = jnp.where(
        channel == magnet.shape[0],
        grain_ids.astype(jnp.float32)[None],
        jnp.pad(magnet, ((0, 1), (0, 0), (0, 0), (0, 0))),
    )
    wide = widen(data, halo, halo, 1, 2)
    m0, m1, m2 = wide[0], wide[1], wide[2]
    exch_coef = lookup(grain_ids, exch_table)

    hs = halo - 1
    ex = slice(1, 1 + cells_x + 2 * hs)
    ey = slice(1, 1 + cells_y + 2 * hs)
    m2p = zpad(m2[ex, ey])
    diverge = (
        m0[2 : 2 + cells_x + 2 * hs, ey]
        - m0[0 : cells_x + 2 * hs, ey]
        + m1[ex, 2 : 2 + cells_y + 2 * hs]
        - m1[ex, 0 : cells_y + 2 * hs]
        + m2p[:, :, 2:]
        - m2p[:, :, :-2]
    ) * 0.5
    sat_w = lookup(wide[3, ex, ey].astype(jnp.int32), sat_table)
    source = -sat_w * diverge

    scalar = jnp.where(inside(hs), source / DIAG, 0.0)
    for sweep in range(1, SWEEPS):
        h = hs - sweep
        off = hs - h
        src = source[off : off + cells_x + 2 * h, off : off + cells_y + 2 * h]
        value = (near_sum(scalar) + src) / DIAG
        scalar = jnp.where(inside(h), value, 0.0) if h > 0 else value

    mag_1 = wide[0:3, halo - 1 : halo + 1 + cells_x, halo - 1 : halo + 1 + cells_y]
    laplace = near_sum(mag_1) - 6.0 * magnet

    node_map = surface_map[:, 0, :]
    cell_ids = jnp.arange(cells_x * cells_y, dtype=jnp.int32)
    onehot = node_map[:, :, None] == cell_ids[None, None, :]
    face_vals = jnp.stack([scalar[:, :, 0], scalar[:, :, -1]]).reshape(2, cells_x * cells_y)
    panels = jnp.sum(jnp.where(onehot, face_vals[:, None, :], 0.0), axis=2)
    low_panels = panels.astype(jnp.bfloat16)
    local_list = near_list[0]
    blank_pick = jnp.zeros((local_list.shape[0], local_list.shape[1], NODES), jnp.bfloat16)
    group = lax.axis_size("gy")
    copies = jnp.broadcast_to(low_panels[None], (group,) + low_panels.shape)
    piece = lax.all_to_all(copies, "gy", 0, 0, tiled=True).reshape(group * 2, NODES)
    valid = (local_list >= 0) & (local_list < piece.shape[0])
    picked = piece[jnp.clip(local_list, 0, piece.shape[0] - 1)]
    chosen = jnp.where(valid[:, :, None], picked, blank_pick)
    double = (
        jnp.einsum("tkij,tkj->ti", near_blocks[0], chosen, preferred_element_type=jnp.float32)
        - 0.5 * panels
    )
    cells = jnp.sum(jnp.where(onehot, double[:, :, None], 0.0), axis=1)
    planes = cells.reshape(2, cells_x, cells_y)

    he = EXT_SWEEPS + 1
    (p_lo, s_lo), (p_hi, s_hi) = swap(
        "gx",
        [planes[:, cells_x - he :], scalar[cells_x - 1 :]],
        [planes[:, :he], scalar[:1]],
    )
    planes_x = jnp.concatenate([p_lo, planes, p_hi], axis=1)
    (q_lo, t_lo), (q_hi, t_hi) = swap(
        "gy",
        [planes_x[:, :, cells_y - he :], scalar[:, cells_y - 1 :]],
        [planes_x[:, :, :he], scalar[:, :1]],
    )
    planes_w = jnp.concatenate([q_lo, planes_x, q_hi], axis=2)

    column = jnp.concatenate([s_lo, scalar, s_hi], axis=0)
    row_pad = ((1, 1), (0, 0), (0, 0))
    scalar_1 = jnp.concatenate([jnp.pad(t_lo, row_pad), column, jnp.pad(t_hi, row_pad)], axis=1)

    z_ids = jnp.arange(cells_z, dtype=jnp.int32)
    bottom = z_ids == 0
    top = z_ids == cells_z - 1

    def reset(values, off, size_x, size_y):
        sub = planes_w[:, off : off + size_x, off : off + size_y]
        return jnp.where(bottom, sub[0][..., None], jnp.where(top, sub[1][..., None], values))

    extend = reset(
        jnp.zeros(planes_w.shape[1:] + (cells_z,), jnp.float32),
        0,
        planes_w.shape[1],
        planes_w.shape[2],
    )
    for sweep in range(EXT_SWEEPS):
        h = he - 1 - sweep
        off = he - h
        value = jnp.where(inside(h), near_sum(extend) / DIAG, 0.0)
        extend = reset(value, off, cells_x + 2 * h, cells_y + 2 * h)

    potential_1 = scalar_1 + extend
    potential = potential_1[1:-1, 1:-1]
    padded = zpad(potential_1)
    grad_x = (potential_1[2:, 1:-1] - potential_1[:-2, 1:-1]) * 0.5
    grad_y = (potential_1[1:-1, 2:] - potential_1[1:-1, :-2]) * 0.5
    grad_z = (padded[1:-1, 1:-1, 2:] - padded[1:-1, 1:-1, :-2]) * 0.5
    field = exch_coef[None] * laplace - jnp.stack([grad_x, grad_y, grad_z])
    return (field, potential)


def solution(mesh):
    return jax.shard_map(
        body,
        mesh=mesh,
        in_specs=(
            P(None, "gx", "gy", None),
            P("gx", "gy", None),
            P(),
            P(),
            P("gx", "gy", None),
            P("gx", "gy", None),
            P("gx", "gy", None, None, None),
        ),
        out_specs=(P(None, "gx", "gy", None), P("gx", "gy", None)),
        check_vma=False,
    )
```

```python
import jax
import jax.numpy as jnp
from jax import lax
from jax.sharding import PartitionSpec as P

NODES = 128
SWEEPS = 8
EXT_SWEEPS = 4
NMAT = 4


SCREEN = 0.25
DIAG = 6.0 + SCREEN


def _pairs(count, step):
    return [(i, i + step) for i in range(count) if 0 <= i + step < count]


def _pack(arrays):
    return jnp.concatenate([a.reshape(-1) for a in arrays])


def _unpack(flat, like):
    out = []
    start = 0
    for a in like:
        out.append(flat[start : start + a.size].reshape(a.shape))
        start += a.size
    return out


def swap(axis, to_next, to_prev):
    count = lax.axis_size(axis)
    if len(to_next) == 1:
        from_prev = [lax.ppermute(to_next[0], axis, _pairs(count, 1))]
        from_next = [lax.ppermute(to_prev[0], axis, _pairs(count, -1))]
        return from_prev, from_next
    from_prev = lax.ppermute(_pack(to_next), axis, _pairs(count, 1))
    from_next = lax.ppermute(_pack(to_prev), axis, _pairs(count, -1))
    return _unpack(from_prev, to_next), _unpack(from_next, to_prev)


def widen(block, hx, hy, dx, dy):
    size_x = block.shape[dx]
    (lo,), (hi,) = swap(
        "gx",
        [lax.slice_in_dim(block, size_x - hx, size_x, axis=dx)],
        [lax.slice_in_dim(block, 0, hx, axis=dx)],
    )
    size_y = block.shape[dy]
    parts = (lo, block, hi)
    (y_lo,), (y_hi,) = swap(
        "gy",
        [jnp.concatenate([lax.slice_in_dim(p, size_y - hy, size_y, axis=dy) for p in parts], axis=dx)],
        [jnp.concatenate([lax.slice_in_dim(p, 0, hy, axis=dy) for p in parts], axis=dx)],
    )
    block = jnp.concatenate(parts, axis=dx)
    return jnp.concatenate([y_lo, block, y_hi], axis=dy)


def zpad(a):
    return jnp.pad(a, [(0, 0)] * (a.ndim - 1) + [(1, 1)])


def near_sum(wide):
    padded = zpad(wide)
    total = wide[..., 2:, 1:-1, :] + wide[..., :-2, 1:-1, :]
    total = total + wide[..., 1:-1, 2:, :] + wide[..., 1:-1, :-2, :]
    total = total + padded[..., 1:-1, 1:-1, 2:] + padded[..., 1:-1, 1:-1, :-2]
    return total


def lookup(grain_ids, table):
    result = jnp.full(grain_ids.shape, table[NMAT - 1], jnp.float32)
    for index in range(NMAT - 2, -1, -1):
        result = jnp.where(grain_ids == index, table[index], result)
    return result


def body(magnet, grain_ids, exch_table, sat_table, surface_map, near_list, near_blocks):
    cells_x = magnet.shape[1]
    cells_y = magnet.shape[2]
    cells_z = magnet.shape[3]
    grid_x = cells_x * lax.axis_size("gx")
    grid_y = cells_y * lax.axis_size("gy")
    base_x = lax.axis_index("gx") * cells_x
    base_y = lax.axis_index("gy") * cells_y

    def inside(h):
        xs = base_x - h + jnp.arange(cells_x + 2 * h, dtype=jnp.int32)
        ys = base_y - h + jnp.arange(cells_y + 2 * h, dtype=jnp.int32)
        ok_x = (xs >= 0) & (xs < grid_x)
        ok_y = (ys >= 0) & (ys < grid_y)
        return (ok_x[:, None] & ok_y[None, :])[:, :, None]

    halo = SWEEPS
    channel = lax.broadcasted_iota(jnp.int32, (magnet.shape[0] + 1,) + magnet.shape[1:], 0)
    data = jnp.where(
        channel == magnet.shape[0],
        grain_ids.astype(jnp.float32)[None],
        jnp.pad(magnet, ((0, 1), (0, 0), (0, 0), (0, 0))),
    )
    wide = widen(data, halo, halo, 1, 2)
    m0, m1, m2 = wide[0], wide[1], wide[2]
    exch_coef = lookup(grain_ids, exch_table)

    hs = halo - 1
    ex = slice(1, 1 + cells_x + 2 * hs)
    ey = slice(1, 1 + cells_y + 2 * hs)
    m2p = zpad(m2[ex, ey])
    diverge = (
        m0[2 : 2 + cells_x + 2 * hs, ey]
        - m0[0 : cells_x + 2 * hs, ey]
        + m1[ex, 2 : 2 + cells_y + 2 * hs]
        - m1[ex, 0 : cells_y + 2 * hs]
        + m2p[:, :, 2:]
        - m2p[:, :, :-2]
    ) * 0.5
    sat_w = lookup(wide[3, ex, ey].astype(jnp.int32), sat_table)
    source = -sat_w * diverge

    scalar = jnp.where(inside(hs), source / DIAG, 0.0)
    for sweep in range(1, SWEEPS):
        h = hs - sweep
        off = hs - h
        src = source[off : off + cells_x + 2 * h, off : off + cells_y + 2 * h]
        value = (near_sum(scalar) + src) / DIAG
        scalar = jnp.where(inside(h), value, 0.0) if h > 0 else value

    mag_1 = wide[0:3, halo - 1 : halo + 1 + cells_x, halo - 1 : halo + 1 + cells_y]
    laplace = near_sum(mag_1) - 6.0 * magnet

    node_map = surface_map[:, 0, :]
    cell_ids = jnp.arange(cells_x * cells_y, dtype=jnp.int32)
    onehot = node_map[:, :, None] == cell_ids[None, None, :]
    face_vals = jnp.stack([scalar[:, :, 0], scalar[:, :, -1]]).reshape(2, cells_x * cells_y)
    panels = jnp.sum(jnp.where(onehot, face_vals[:, None, :], 0.0), axis=2)
    low_panels = panels.astype(jnp.bfloat16)
    local_list = near_list[0]
    blank_pick = jnp.zeros((local_list.shape[0], local_list.shape[1], NODES), jnp.bfloat16)
    group = lax.axis_size("gy")
    copies = jnp.broadcast_to(low_panels[None], (group,) + low_panels.shape)
    piece = lax.all_to_all(copies, "gy", 0, 0, tiled=True).reshape(group * 2, NODES)
    valid = (local_list >= 0) & (local_list < piece.shape[0])
    picked = piece[jnp.clip(local_list, 0, piece.shape[0] - 1)]
    chosen = jnp.where(valid[:, :, None], picked, blank_pick)
    double = (
        jnp.einsum("tkij,tkj->ti", near_blocks[0], chosen, preferred_element_type=jnp.float32)
        - 0.5 * panels
    )
    cells = jnp.sum(jnp.where(onehot, double[:, :, None], 0.0), axis=1)
    planes = cells.reshape(2, cells_x, cells_y)

    he = EXT_SWEEPS + 1
    (p_lo, s_lo), (p_hi, s_hi) = swap(
        "gx",
        [planes[:, cells_x - he :], scalar[cells_x - 1 :]],
        [planes[:, :he], scalar[:1]],
    )
    planes_x = jnp.concatenate([p_lo, planes, p_hi], axis=1)
    (q_lo, t_lo), (q_hi, t_hi) = swap(
        "gy",
        [planes_x[:, :, cells_y - he :], scalar[:, cells_y - 1 :]],
        [planes_x[:, :, :he], scalar[:, :1]],
    )
    planes_w = jnp.concatenate([q_lo, planes_x, q_hi], axis=2)

    column = jnp.concatenate([s_lo, scalar, s_hi], axis=0)
    row_pad = ((1, 1), (0, 0), (0, 0))
    scalar_1 = jnp.concatenate([jnp.pad(t_lo, row_pad), column, jnp.pad(t_hi, row_pad)], axis=1)

    z_ids = jnp.arange(cells_z, dtype=jnp.int32)
    bottom = z_ids == 0
    top = z_ids == cells_z - 1

    def reset(values, off, size_x, size_y):
        sub = planes_w[:, off : off + size_x, off : off + size_y]
        return jnp.where(bottom, sub[0][..., None], jnp.where(top, sub[1][..., None], values))

    extend = reset(
        jnp.zeros(planes_w.shape[1:] + (cells_z,), jnp.float32),
        0,
        planes_w.shape[1],
        planes_w.shape[2],
    )
    for sweep in range(EXT_SWEEPS):
        h = he - 1 - sweep
        off = he - h
        value = jnp.where(inside(h), near_sum(extend) / DIAG, 0.0)
        extend = reset(value, off, cells_x + 2 * h, cells_y + 2 * h)

    potential_1 = scalar_1 + extend
    potential = potential_1[1:-1, 1:-1]
    padded = zpad(potential_1)
    grad_x = (potential_1[2:, 1:-1] - potential_1[:-2, 1:-1]) * 0.5
    grad_y = (potential_1[1:-1, 2:] - potential_1[1:-1, :-2]) * 0.5
    grad_z = (padded[1:-1, 1:-1, 2:] - padded[1:-1, 1:-1, :-2]) * 0.5
    field = exch_coef[None] * laplace - jnp.stack([grad_x, grad_y, grad_z])
    return (field, potential)


def solution(mesh):
    return jax.shard_map(
        body,
        mesh=mesh,
        in_specs=(
            P(None, "gx", "gy", None),
            P("gx", "gy", None),
            P(),
            P(),
            P("gx", "gy", None),
            P("gx", "gy", None),
            P("gx", "gy", None, None, None),
        ),
        out_specs=(P(None, "gx", "gy", None), P("gx", "gy", None)),
        check_vma=False,
    )
```

```python
import jax
import jax.numpy as jnp
from jax import lax
from jax.sharding import PartitionSpec as P

NODES = 128
SWEEPS = 8
EXT_SWEEPS = 4
NMAT = 4


SCREEN = 0.25
DIAG = 6.0 + SCREEN


def _pairs(count, step):
    return [(i, i + step) for i in range(count) if 0 <= i + step < count]


def _pack(arrays):
    return jnp.concatenate([a.reshape(-1) for a in arrays])


def _unpack(flat, like):
    out = []
    start = 0
    for a in like:
        out.append(flat[start : start + a.size].reshape(a.shape))
        start += a.size
    return out


def swap(axis, to_next, to_prev):
    count = lax.axis_size(axis)
    if len(to_next) == 1:
        from_prev = [lax.ppermute(to_next[0], axis, _pairs(count, 1))]
        from_next = [lax.ppermute(to_prev[0], axis, _pairs(count, -1))]
        return from_prev, from_next
    from_prev = lax.ppermute(_pack(to_next), axis, _pairs(count, 1))
    from_next = lax.ppermute(_pack(to_prev), axis, _pairs(count, -1))
    return _unpack(from_prev, to_next), _unpack(from_next, to_prev)


def widen(block, hx, hy, dx, dy):
    size_x = block.shape[dx]
    (lo,), (hi,) = swap(
        "gx",
        [lax.slice_in_dim(block, size_x - hx, size_x, axis=dx)],
        [lax.slice_in_dim(block, 0, hx, axis=dx)],
    )
    size_y = block.shape[dy]
    parts = (lo, block, hi)
    (y_lo,), (y_hi,) = swap(
        "gy",
        [jnp.concatenate([lax.slice_in_dim(p, size_y - hy, size_y, axis=dy) for p in parts], axis=dx)],
        [jnp.concatenate([lax.slice_in_dim(p, 0, hy, axis=dy) for p in parts], axis=dx)],
    )
    block = jnp.concatenate(parts, axis=dx)
    return jnp.concatenate([y_lo, block, y_hi], axis=dy)


def zpad(a):
    return jnp.pad(a, [(0, 0)] * (a.ndim - 1) + [(1, 1)])


def near_sum(wide):
    padded = zpad(wide)
    total = wide[..., 2:, 1:-1, :] + wide[..., :-2, 1:-1, :]
    total = total + wide[..., 1:-1, 2:, :] + wide[..., 1:-1, :-2, :]
    total = total + padded[..., 1:-1, 1:-1, 2:] + padded[..., 1:-1, 1:-1, :-2]
    return total


def lookup(grain_ids, table):
    result = jnp.full(grain_ids.shape, table[NMAT - 1], jnp.float32)
    for index in range(NMAT - 2, -1, -1):
        result = jnp.where(grain_ids == index, table[index], result)
    return result


def body(magnet, grain_ids, exch_table, sat_table, surface_map, near_list, near_blocks):
    cells_x = magnet.shape[1]
    cells_y = magnet.shape[2]
    cells_z = magnet.shape[3]
    grid_x = cells_x * lax.axis_size("gx")
    grid_y = cells_y * lax.axis_size("gy")
    base_x = lax.axis_index("gx") * cells_x
    base_y = lax.axis_index("gy") * cells_y

    def inside(h):
        xs = base_x - h + jnp.arange(cells_x + 2 * h, dtype=jnp.int32)
        ys = base_y - h + jnp.arange(cells_y + 2 * h, dtype=jnp.int32)
        ok_x = (xs >= 0) & (xs < grid_x)
        ok_y = (ys >= 0) & (ys < grid_y)
        return (ok_x[:, None] & ok_y[None, :])[:, :, None]

    halo = SWEEPS
    channel = lax.broadcasted_iota(jnp.int32, (magnet.shape[0] + 1,) + magnet.shape[1:], 0)
    data = jnp.where(
        channel == magnet.shape[0],
        grain_ids.astype(jnp.float32)[None],
        jnp.pad(magnet, ((0, 1), (0, 0), (0, 0), (0, 0))),
    )
    wide = widen(data, halo, halo, 1, 2)
    m0, m1, m2 = wide[0], wide[1], wide[2]
    exch_coef = lookup(grain_ids, exch_table)

    hs = halo - 1
    ex = slice(1, 1 + cells_x + 2 * hs)
    ey = slice(1, 1 + cells_y + 2 * hs)
    m2p = zpad(m2[ex, ey])
    diverge = (
        m0[2 : 2 + cells_x + 2 * hs, ey]
        - m0[0 : cells_x + 2 * hs, ey]
        + m1[ex, 2 : 2 + cells_y + 2 * hs]
        - m1[ex, 0 : cells_y + 2 * hs]
        + m2p[:, :, 2:]
        - m2p[:, :, :-2]
    ) * 0.5
    sat_w = lookup(wide[3, ex, ey].astype(jnp.int32), sat_table)
    source = -sat_w * diverge

    scalar = jnp.where(inside(hs), source / DIAG, 0.0)
    for sweep in range(1, SWEEPS):
        h = hs - sweep
        off = hs - h
        src = source[off : off + cells_x + 2 * h, off : off + cells_y + 2 * h]
        value = (near_sum(scalar) + src) / DIAG
        scalar = jnp.where(inside(h), value, 0.0) if h > 0 else value

    mag_1 = wide[0:3, halo - 1 : halo + 1 + cells_x, halo - 1 : halo + 1 + cells_y]
    laplace = near_sum(mag_1) - 6.0 * magnet

    node_map = surface_map[:, 0, :]
    cell_ids = jnp.arange(cells_x * cells_y, dtype=jnp.int32)
    onehot = node_map[:, :, None] == cell_ids[None, None, :]
    face_vals = jnp.stack([scalar[:, :, 0], scalar[:, :, -1]]).reshape(2, cells_x * cells_y)
    panels = jnp.sum(jnp.where(onehot, face_vals[:, None, :], 0.0), axis=2)
    low_panels = panels.astype(jnp.bfloat16)
    local_list = near_list[0]
    blank_pick = jnp.zeros((local_list.shape[0], local_list.shape[1], NODES), jnp.bfloat16)
    group = lax.axis_size("gy")
    copies = jnp.sum(
        jnp.where(
            jnp.broadcast_to(onehot[None], (group,) + onehot.shape),
            face_vals[None, :, None, :],
            0.0,
        ),
        axis=3,
    ).astype(jnp.bfloat16)
    piece = lax.all_to_all(copies, "gy", 0, 0, tiled=True).reshape(group * 2, NODES)
    valid = (local_list >= 0) & (local_list < piece.shape[0])
    picked = piece[jnp.clip(local_list, 0, piece.shape[0] - 1)]
    chosen = jnp.where(valid[:, :, None], picked, blank_pick)
    double = (
        jnp.einsum("tkij,tkj->ti", near_blocks[0], chosen, preferred_element_type=jnp.float32)
        - 0.5 * panels
    )
    cells = jnp.sum(jnp.where(onehot, double[:, :, None], 0.0), axis=1)
    planes = cells.reshape(2, cells_x, cells_y)

    he = EXT_SWEEPS + 1
    (p_lo, s_lo), (p_hi, s_hi) = swap(
        "gx",
        [planes[:, cells_x - he :], scalar[cells_x - 1 :]],
        [planes[:, :he], scalar[:1]],
    )
    planes_x = jnp.concatenate([p_lo, planes, p_hi], axis=1)
    (q_lo, t_lo), (q_hi, t_hi) = swap(
        "gy",
        [planes_x[:, :, cells_y - he :], scalar[:, cells_y - 1 :]],
        [planes_x[:, :, :he], scalar[:, :1]],
    )
    planes_w = jnp.concatenate([q_lo, planes_x, q_hi], axis=2)

    column = jnp.concatenate([s_lo, scalar, s_hi], axis=0)
    row_pad = ((1, 1), (0, 0), (0, 0))
    scalar_1 = jnp.concatenate([jnp.pad(t_lo, row_pad), column, jnp.pad(t_hi, row_pad)], axis=1)

    z_ids = jnp.arange(cells_z, dtype=jnp.int32)
    bottom = z_ids == 0
    top = z_ids == cells_z - 1

    def reset(values, off, size_x, size_y):
        sub = planes_w[:, off : off + size_x, off : off + size_y]
        return jnp.where(bottom, sub[0][..., None], jnp.where(top, sub[1][..., None], values))

    extend = reset(
        jnp.zeros(planes_w.shape[1:] + (cells_z,), jnp.float32),
        0,
        planes_w.shape[1],
        planes_w.shape[2],
    )
    for sweep in range(EXT_SWEEPS):
        h = he - 1 - sweep
        off = he - h
        value = jnp.where(inside(h), near_sum(extend) / DIAG, 0.0)
        extend = reset(value, off, cells_x + 2 * h, cells_y + 2 * h)

    potential_1 = scalar_1 + extend
    potential = potential_1[1:-1, 1:-1]
    padded = zpad(potential_1)
    grad_x = (potential_1[2:, 1:-1] - potential_1[:-2, 1:-1]) * 0.5
    grad_y = (potential_1[1:-1, 2:] - potential_1[1:-1, :-2]) * 0.5
    grad_z = (padded[1:-1, 1:-1, 2:] - padded[1:-1, 1:-1, :-2]) * 0.5
    field = exch_coef[None] * laplace - jnp.stack([grad_x, grad_y, grad_z])
    return (field, potential)


def solution(mesh):
    return jax.shard_map(
        body,
        mesh=mesh,
        in_specs=(
            P(None, "gx", "gy", None),
            P("gx", "gy", None),
            P(),
            P(),
            P("gx", "gy", None),
            P("gx", "gy", None),
            P("gx", "gy", None, None, None),
        ),
        out_specs=(P(None, "gx", "gy", None), P("gx", "gy", None)),
        check_vma=False,
    )
```

```python
import jax
import jax.numpy as jnp
from jax import lax
from jax.sharding import PartitionSpec as P

NODES = 128
SWEEPS = 8
EXT_SWEEPS = 4
NMAT = 4


SCREEN = 0.25
DIAG = 6.0 + SCREEN


def _pairs(count, step):
    return [(i, i + step) for i in range(count) if 0 <= i + step < count]


def _pack(arrays):
    return jnp.concatenate([a.reshape(-1) for a in arrays])


def _unpack(flat, like):
    out = []
    start = 0
    for a in like:
        out.append(flat[start : start + a.size].reshape(a.shape))
        start += a.size
    return out


def swap(axis, to_next, to_prev):
    count = lax.axis_size(axis)
    if len(to_next) == 1:
        from_prev = [lax.ppermute(to_next[0], axis, _pairs(count, 1))]
        from_next = [lax.ppermute(to_prev[0], axis, _pairs(count, -1))]
        return from_prev, from_next
    from_prev = lax.ppermute(_pack(to_next), axis, _pairs(count, 1))
    from_next = lax.ppermute(_pack(to_prev), axis, _pairs(count, -1))
    return _unpack(from_prev, to_next), _unpack(from_next, to_prev)


def widen(block, hx, hy, dx, dy):
    size_x = block.shape[dx]
    (lo,), (hi,) = swap(
        "gx",
        [lax.slice_in_dim(block, size_x - hx, size_x, axis=dx)],
        [lax.slice_in_dim(block, 0, hx, axis=dx)],
    )
    size_y = block.shape[dy]
    parts = (lo, block, hi)
    (y_lo,), (y_hi,) = swap(
        "gy",
        [jnp.concatenate([lax.slice_in_dim(p, size_y - hy, size_y, axis=dy) for p in parts], axis=dx)],
        [jnp.concatenate([lax.slice_in_dim(p, 0, hy, axis=dy) for p in parts], axis=dx)],
    )
    block = jnp.concatenate(parts, axis=dx)
    return jnp.concatenate([y_lo, block, y_hi], axis=dy)


def zpad(a):
    return jnp.pad(a, [(0, 0)] * (a.ndim - 1) + [(1, 1)])


def near_sum(wide):
    padded = zpad(wide)
    total = wide[..., 2:, 1:-1, :] + wide[..., :-2, 1:-1, :]
    total = total + wide[..., 1:-1, 2:, :] + wide[..., 1:-1, :-2, :]
    total = total + padded[..., 1:-1, 1:-1, 2:] + padded[..., 1:-1, 1:-1, :-2]
    return total


def lookup(grain_ids, table):
    result = jnp.full(grain_ids.shape, table[NMAT - 1], jnp.float32)
    for index in range(NMAT - 2, -1, -1):
        result = jnp.where(grain_ids == index, table[index], result)
    return result


def body(magnet, grain_ids, exch_table, sat_table, surface_map, near_list, near_blocks):
    cells_x = magnet.shape[1]
    cells_y = magnet.shape[2]
    cells_z = magnet.shape[3]
    grid_x = cells_x * lax.axis_size("gx")
    grid_y = cells_y * lax.axis_size("gy")
    base_x = lax.axis_index("gx") * cells_x
    base_y = lax.axis_index("gy") * cells_y

    def inside(h):
        xs = base_x - h + jnp.arange(cells_x + 2 * h, dtype=jnp.int32)
        ys = base_y - h + jnp.arange(cells_y + 2 * h, dtype=jnp.int32)
        ok_x = (xs >= 0) & (xs < grid_x)
        ok_y = (ys >= 0) & (ys < grid_y)
        return (ok_x[:, None] & ok_y[None, :])[:, :, None]

    halo = SWEEPS
    channel = lax.broadcasted_iota(jnp.int32, (magnet.shape[0] + 1,) + magnet.shape[1:], 0)
    data = jnp.where(
        channel == magnet.shape[0],
        grain_ids.astype(jnp.float32)[None],
        jnp.pad(magnet, ((0, 1), (0, 0), (0, 0), (0, 0))),
    )
    wide = widen(data, halo, halo, 1, 2)
    m0, m1, m2 = wide[0], wide[1], wide[2]
    exch_coef = lookup(grain_ids, exch_table)

    hs = halo - 1
    ex = slice(1, 1 + cells_x + 2 * hs)
    ey = slice(1, 1 + cells_y + 2 * hs)
    m2p = zpad(m2[ex, ey])
    diverge = (
        m0[2 : 2 + cells_x + 2 * hs, ey]
        - m0[0 : cells_x + 2 * hs, ey]
        + m1[ex, 2 : 2 + cells_y + 2 * hs]
        - m1[ex, 0 : cells_y + 2 * hs]
        + m2p[:, :, 2:]
        - m2p[:, :, :-2]
    ) * 0.5
    sat_w = lookup(wide[3, ex, ey].astype(jnp.int32), sat_table)
    source = -sat_w * diverge

    scalar = jnp.where(inside(hs), source / DIAG, 0.0)
    for sweep in range(1, SWEEPS):
        h = hs - sweep
        off = hs - h
        src = source[off : off + cells_x + 2 * h, off : off + cells_y + 2 * h]
        value = (near_sum(scalar) + src) / DIAG
        scalar = jnp.where(inside(h), value, 0.0) if h > 0 else value

    mag_1 = wide[0:3, halo - 1 : halo + 1 + cells_x, halo - 1 : halo + 1 + cells_y]
    laplace = near_sum(mag_1) - 6.0 * magnet

    node_map = surface_map[:, 0, :]
    cell_ids = jnp.arange(cells_x * cells_y, dtype=jnp.int32)
    onehot = node_map[:, :, None] == cell_ids[None, None, :]
    face_vals = jnp.stack([scalar[:, :, 0], scalar[:, :, -1]]).reshape(2, cells_x * cells_y)
    panels = jnp.sum(jnp.where(onehot, face_vals[:, None, :], 0.0), axis=2)
    low_panels = panels.astype(jnp.bfloat16)
    local_list = near_list[0]
    blank_pick = jnp.zeros((local_list.shape[0], local_list.shape[1], NODES), jnp.bfloat16)
    group = lax.axis_size("gy")
    copies = jnp.broadcast_to(low_panels[None], (group,) + low_panels.shape)
    piece = lax.all_to_all(copies, "gy", 0, 0, tiled=True).reshape(group * 2, NODES)
    valid = (local_list >= 0) & (local_list < piece.shape[0])
    picked = piece[jnp.clip(local_list, 0, piece.shape[0] - 1)]
    chosen = jnp.where(valid[:, :, None], picked, blank_pick)
    double = (
        jnp.einsum("tkij,tkj->ti", near_blocks[0], chosen, preferred_element_type=jnp.float32)
        - 0.5 * panels
    )
    cells = jnp.sum(jnp.where(onehot, double[:, :, None], 0.0), axis=1)
    planes = cells.reshape(2, cells_x, cells_y)

    he = EXT_SWEEPS + 1
    (p_lo, s_lo), (p_hi, s_hi) = swap(
        "gx",
        [planes[:, cells_x - he :], scalar[cells_x - 1 :]],
        [planes[:, :he], scalar[:1]],
    )
    pieces = (p_lo, planes, p_hi)
    (q_lo, t_lo), (q_hi, t_hi) = swap(
        "gy",
        [jnp.concatenate([p[:, :, cells_y - he :] for p in pieces], axis=1), scalar[:, cells_y - 1 :]],
        [jnp.concatenate([p[:, :, :he] for p in pieces], axis=1), scalar[:, :1]],
    )
    planes_x = jnp.concatenate(pieces, axis=1)
    planes_w = jnp.concatenate([q_lo, planes_x, q_hi], axis=2)

    column = jnp.concatenate([s_lo, scalar, s_hi], axis=0)
    row_pad = ((1, 1), (0, 0), (0, 0))
    scalar_1 = jnp.concatenate([jnp.pad(t_lo, row_pad), column, jnp.pad(t_hi, row_pad)], axis=1)

    z_ids = jnp.arange(cells_z, dtype=jnp.int32)
    bottom = z_ids == 0
    top = z_ids == cells_z - 1

    def reset(values, off, size_x, size_y):
        sub = planes_w[:, off : off + size_x, off : off + size_y]
        return jnp.where(bottom, sub[0][..., None], jnp.where(top, sub[1][..., None], values))

    extend = reset(
        jnp.zeros(planes_w.shape[1:] + (cells_z,), jnp.float32),
        0,
        planes_w.shape[1],
        planes_w.shape[2],
    )
    for sweep in range(EXT_SWEEPS):
        h = he - 1 - sweep
        off = he - h
        value = jnp.where(inside(h), near_sum(extend) / DIAG, 0.0)
        extend = reset(value, off, cells_x + 2 * h, cells_y + 2 * h)

    potential_1 = scalar_1 + extend
    potential = potential_1[1:-1, 1:-1]
    padded = zpad(potential_1)
    grad_x = (potential_1[2:, 1:-1] - potential_1[:-2, 1:-1]) * 0.5
    grad_y = (potential_1[1:-1, 2:] - potential_1[1:-1, :-2]) * 0.5
    grad_z = (padded[1:-1, 1:-1, 2:] - padded[1:-1, 1:-1, :-2]) * 0.5
    field = exch_coef[None] * laplace - jnp.stack([grad_x, grad_y, grad_z])
    return (field, potential)


def solution(mesh):
    return jax.shard_map(
        body,
        mesh=mesh,
        in_specs=(
            P(None, "gx", "gy", None),
            P("gx", "gy", None),
            P(),
            P(),
            P("gx", "gy", None),
            P("gx", "gy", None),
            P("gx", "gy", None, None, None),
        ),
        out_specs=(P(None, "gx", "gy", None), P("gx", "gy", None)),
        check_vma=False,
    )
```

```python
import jax
import jax.numpy as jnp
from jax import lax
from jax.sharding import PartitionSpec as P

NODES = 128
SWEEPS = 8
EXT_SWEEPS = 4
NMAT = 4


SCREEN = 0.25
DIAG = 6.0 + SCREEN


def _pairs(count, step):
    return [(i, i + step) for i in range(count) if 0 <= i + step < count]


def _pack(arrays):
    return jnp.concatenate([a.reshape(-1) for a in arrays])


def _unpack(flat, like):
    out = []
    start = 0
    for a in like:
        out.append(flat[start : start + a.size].reshape(a.shape))
        start += a.size
    return out


def swap(axis, to_next, to_prev):
    count = lax.axis_size(axis)
    if len(to_next) == 1:
        from_prev = [lax.ppermute(to_next[0], axis, _pairs(count, 1))]
        from_next = [lax.ppermute(to_prev[0], axis, _pairs(count, -1))]
        return from_prev, from_next
    from_prev = lax.ppermute(_pack(to_next), axis, _pairs(count, 1))
    from_next = lax.ppermute(_pack(to_prev), axis, _pairs(count, -1))
    return _unpack(from_prev, to_next), _unpack(from_next, to_prev)


def widen(block, hx, hy, dx, dy):
    size_x = block.shape[dx]
    (lo,), (hi,) = swap(
        "gx",
        [lax.slice_in_dim(block, size_x - hx, size_x, axis=dx)],
        [lax.slice_in_dim(block, 0, hx, axis=dx)],
    )
    size_y = block.shape[dy]
    parts = (lo, block, hi)
    (y_lo,), (y_hi,) = swap(
        "gy",
        [jnp.concatenate([lax.slice_in_dim(p, size_y - hy, size_y, axis=dy) for p in parts], axis=dx)],
        [jnp.concatenate([lax.slice_in_dim(p, 0, hy, axis=dy) for p in parts], axis=dx)],
    )
    block = jnp.concatenate(parts, axis=dx)
    return jnp.concatenate([y_lo, block, y_hi], axis=dy)


def zpad(a):
    return jnp.pad(a, [(0, 0)] * (a.ndim - 1) + [(1, 1)])


def near_sum(wide):
    padded = zpad(wide)
    total = wide[..., 2:, 1:-1, :] + wide[..., :-2, 1:-1, :]
    total = total + wide[..., 1:-1, 2:, :] + wide[..., 1:-1, :-2, :]
    total = total + padded[..., 1:-1, 1:-1, 2:] + padded[..., 1:-1, 1:-1, :-2]
    return total


def lookup(grain_ids, table):
    result = jnp.full(grain_ids.shape, table[NMAT - 1], jnp.float32)
    for index in range(NMAT - 2, -1, -1):
        result = jnp.where(grain_ids == index, table[index], result)
    return result


def body(magnet, grain_ids, exch_table, sat_table, surface_map, near_list, near_blocks):
    cells_x = magnet.shape[1]
    cells_y = magnet.shape[2]
    cells_z = magnet.shape[3]
    grid_x = cells_x * lax.axis_size("gx")
    grid_y = cells_y * lax.axis_size("gy")
    base_x = lax.axis_index("gx") * cells_x
    base_y = lax.axis_index("gy") * cells_y

    def inside(h):
        xs = base_x - h + jnp.arange(cells_x + 2 * h, dtype=jnp.int32)
        ys = base_y - h + jnp.arange(cells_y + 2 * h, dtype=jnp.int32)
        ok_x = (xs >= 0) & (xs < grid_x)
        ok_y = (ys >= 0) & (ys < grid_y)
        return (ok_x[:, None] & ok_y[None, :])[:, :, None]

    halo = SWEEPS
    channel = lax.broadcasted_iota(jnp.int32, (magnet.shape[0] + 1,) + magnet.shape[1:], 0)
    data = jnp.where(
        channel == magnet.shape[0],
        grain_ids.astype(jnp.float32)[None],
        jnp.pad(magnet, ((0, 1), (0, 0), (0, 0), (0, 0))),
    )
    wide = widen(data, halo, halo, 1, 2)
    m0, m1, m2 = wide[0], wide[1], wide[2]
    exch_coef = lookup(grain_ids, exch_table)

    hs = halo - 1
    ex = slice(1, 1 + cells_x + 2 * hs)
    ey = slice(1, 1 + cells_y + 2 * hs)
    m2p = zpad(m2[ex, ey])
    diverge = (
        m0[2 : 2 + cells_x + 2 * hs, ey]
        - m0[0 : cells_x + 2 * hs, ey]
        + m1[ex, 2 : 2 + cells_y + 2 * hs]
        - m1[ex, 0 : cells_y + 2 * hs]
        + m2p[:, :, 2:]
        - m2p[:, :, :-2]
    ) * 0.5
    sat_w = lookup(wide[3, ex, ey].astype(jnp.int32), sat_table)
    source = -sat_w * diverge

    scalar = jnp.where(inside(hs), source / DIAG, 0.0)
    for sweep in range(1, SWEEPS):
        h = hs - sweep
        off = hs - h
        src = source[off : off + cells_x + 2 * h, off : off + cells_y + 2 * h]
        value = (near_sum(scalar) + src) / DIAG
        scalar = jnp.where(inside(h), value, 0.0) if h > 0 else value

    mag_1 = wide[0:3, halo - 1 : halo + 1 + cells_x, halo - 1 : halo + 1 + cells_y]
    laplace = near_sum(mag_1) - 6.0 * magnet

    node_map = surface_map[:, 0, :]
    cell_ids = jnp.arange(cells_x * cells_y, dtype=jnp.int32)
    onehot = node_map[:, :, None] == cell_ids[None, None, :]
    face_vals = jnp.stack([scalar[:, :, 0], scalar[:, :, -1]]).reshape(2, cells_x * cells_y)
    panels = jnp.sum(jnp.where(onehot, face_vals[:, None, :], 0.0), axis=2)
    low_panels = panels.astype(jnp.bfloat16)
    local_list = near_list[0]
    group = lax.axis_size("gy")
    copies = jnp.broadcast_to(low_panels[None], (group,) + low_panels.shape)
    piece = lax.all_to_all(copies, "gy", 0, 0, tiled=True).reshape(group * 2, NODES)
    chosen = piece[jnp.clip(local_list, 0, piece.shape[0] - 1)]
    double = (
        jnp.einsum("tkij,tkj->ti", near_blocks[0], chosen, preferred_element_type=jnp.float32)
        - 0.5 * panels
    )
    cells = jnp.sum(jnp.where(onehot, double[:, :, None], 0.0), axis=1)
    planes = cells.reshape(2, cells_x, cells_y)

    he = EXT_SWEEPS + 1
    (p_lo, s_lo), (p_hi, s_hi) = swap(
        "gx",
        [planes[:, cells_x - he :], scalar[cells_x - 1 :]],
        [planes[:, :he], scalar[:1]],
    )
    planes_x = jnp.concatenate([p_lo, planes, p_hi], axis=1)
    (q_lo, t_lo), (q_hi, t_hi) = swap(
        "gy",
        [planes_x[:, :, cells_y - he :], scalar[:, cells_y - 1 :]],
        [planes_x[:, :, :he], scalar[:, :1]],
    )
    planes_w = jnp.concatenate([q_lo, planes_x, q_hi], axis=2)

    column = jnp.concatenate([s_lo, scalar, s_hi], axis=0)
    row_pad = ((1, 1), (0, 0), (0, 0))
    scalar_1 = jnp.concatenate([jnp.pad(t_lo, row_pad), column, jnp.pad(t_hi, row_pad)], axis=1)

    z_ids = jnp.arange(cells_z, dtype=jnp.int32)
    bottom = z_ids == 0
    top = z_ids == cells_z - 1

    def reset(values, off, size_x, size_y):
        sub = planes_w[:, off : off + size_x, off : off + size_y]
        return jnp.where(bottom, sub[0][..., None], jnp.where(top, sub[1][..., None], values))

    extend = reset(
        jnp.zeros(planes_w.shape[1:] + (cells_z,), jnp.float32),
        0,
        planes_w.shape[1],
        planes_w.shape[2],
    )
    for sweep in range(EXT_SWEEPS):
        h = he - 1 - sweep
        off = he - h
        value = jnp.where(inside(h), near_sum(extend) / DIAG, 0.0)
        extend = reset(value, off, cells_x + 2 * h, cells_y + 2 * h)

    potential_1 = scalar_1 + extend
    potential = potential_1[1:-1, 1:-1]
    padded = zpad(potential_1)
    grad_x = (potential_1[2:, 1:-1] - potential_1[:-2, 1:-1]) * 0.5
    grad_y = (potential_1[1:-1, 2:] - potential_1[1:-1, :-2]) * 0.5
    grad_z = (padded[1:-1, 1:-1, 2:] - padded[1:-1, 1:-1, :-2]) * 0.5
    field = exch_coef[None] * laplace - jnp.stack([grad_x, grad_y, grad_z])
    return (field, potential)


def solution(mesh):
    return jax.shard_map(
        body,
        mesh=mesh,
        in_specs=(
            P(None, "gx", "gy", None),
            P("gx", "gy", None),
            P(),
            P(),
            P("gx", "gy", None),
            P("gx", "gy", None),
            P("gx", "gy", None, None, None),
        ),
        out_specs=(P(None, "gx", "gy", None), P("gx", "gy", None)),
        check_vma=False,
    )
```
